256 devices in a mesh: seq: 64 (over z, x, core), tensor: 4 (over y).
Axes of the slice: x: 4, y: 4, z: 8, core: 2. Of those that a mesh axis runs over, the one named last changes fastest.
Arguments:
- residual: bfloat16 [16384, 2048], P('seq', 'tensor'), may hold values from -0.29882812 to 0.29882812
- query: bfloat16 [16384, 2048], P('seq', 'tensor'), may hold values from -13 to 13
- new_keys: bfloat16 [16384, 2048], P('seq', 'tensor'), may hold values from -6 to 6
- new_values: bfloat16 [16384, 2048], P('seq', 'tensor'), may hold values from -6 to 6
- leaf_kv: bfloat16 [2, 4096, 2048], P(None, 'seq', 'tensor'), may hold values from -6 to 6
- branch_kv: bfloat16 [2, 4096, 2048], P(None, 'seq', 'tensor'), may hold values from -6 to 6
- root_kv: bfloat16 [2, 2048, 2048], P(None, 'seq', 'tensor'), may hold values from -10 to 10
- out_weight: bfloat16 [2048, 2048], P('tensor'), may hold values from -0.125 to 0.125
- norm_gain: float32 [2048], replicated, may hold values from 0.25 to 1.75
- norm_bias: float32 [2048], replicated, may hold values from -1.8 to 1.8
- up_weight: bfloat16 [2048, 4096], P(None, 'tensor'), may hold values from -0.125 to 0.125
- up_bias: float32 [4096], P('tensor'), may hold values from -3 to 3
- down_weight: bfloat16 [4096, 2048], P('tensor'), may hold values from -0.09375 to 0.09375
- down_bias: float32 [2048], replicated, may hold values from -1.8 to 1.8
- segment: int32 [64], replicated, may hold values from 0 to 15, never falling along the last dimension, each value on 1 to 8 neighbouring positions
- new_len: int32 [64], replicated, may hold values from 1 to 256, 12288 in all
Outputs:
- layer_out: bfloat16 [16384, 2048], P('seq', 'tensor')
The draws below stay inside these ranges and needn't reach their ends.
Inputs may be any that keep to these rules, and one draw needn't show every extreme that they name: `segment`: never falling along the requests, so the requests of one branch node have consecutive indices; every node 0 to 15 has 1 to 8 requests and one has exactly 8. `new_len`: the largest is exactly 256; they sum to 12288.
All inputs are finite; a program needn't handle non-finite values.
Results may differ from the reference program's by a relative error of at most 0.018.
Values may be sent and summed in bfloat16 or wider, within the bound.
No kernel may reach another device: no remote copies, remote signals or barrier semaphores. Data moves between devices by JAX's collectives and lax.ppermute only.
A program may use at most 128 MiB of HBM per device.

```python
import math
import jax
import jax.numpy as jnp
import numpy as np
from jax import lax

D = 2048
HEADS = 16
HD = 128
FF = 4096
NEW = 256
BR = 256
LEAF = 64
REQS = 64
TOKENS = 16384
ROOT = 2048
BRANCHES = 16
SEG_MOST = 8
TOTAL_NEW = 12288


def draw_query(key, part):
    base_key = jax.random.fold_in(key, 11)
    values = 1.5 * jnp.clip(jax.random.normal(base_key, (TOKENS, HEADS * HD), jnp.float32), -6.0, 6.0)
    return values.astype(jnp.bfloat16)


def draw_root_kv(key, part):
    base_key = jax.random.fold_in(key, 23)
    values = jnp.clip(jax.random.normal(base_key, (2, ROOT, HEADS * HD), jnp.float32), -6.0, 6.0)
    return values.astype(jnp.bfloat16)


def shard_levels(key, extent, shards, low, top_value):
    loudness = 1.0
    for axis_at, shards_of in shards:
        draws = jax.random.uniform(jax.random.fold_in(jax.random.fold_in(key, 6), axis_at), (shards_of,), jnp.float32, low / len(shards), top_value / len(shards))
        loudness = loudness * jnp.repeat(jnp.exp(draws), extent[axis_at] // shards_of).reshape((-1,) + (1,) * (len(extent) - 1 - axis_at))
    return loudness


def length_profile(count, total, reach, slope):
    weights = [(1 << 20) // math.isqrt(rank ** slope) + 1 for rank in range(2, count + 1)]
    surplus, given = total - reach - (count - 1), [1] * (count - 1)
    while surplus > 0:
        candidates = [i for i in range(count - 1) if given[i] < reach]
        mass, left = sum([weights[i] for i in candidates]), surplus
        for i in candidates:
            addition = min(reach - given[i], max(1, left * weights[i] // mass), surplus)
            given[i] = given[i] + addition
            surplus = surplus - addition
    return np.array([reach] + given)


def ragged_sizes(key, count, total, most, lean):
    if count == 2:
        one = jax.random.randint(key, (), max(1, total - most), min(most, total - 1) + 1)
        return jnp.stack([one, total - one])
    lengths = jnp.asarray(length_profile(count, total, most, lean), jnp.int32)
    pairs = (count - 1) // 2
    giver, taker = lengths[1:1 + 2 * pairs:2], lengths[2:2 + 2 * pairs:2]
    room = jnp.minimum(giver - 1, most - taker)
    moved = jax.random.randint(jax.random.fold_in(key, 1), (pairs,), 0, 1 << 20) % (room + 1)
    lengths = lengths.at[1:1 + 2 * pairs:2].set(giver - moved).at[2:2 + 2 * pairs:2].set(taker + moved)
    return lengths[jax.random.permutation(jax.random.fold_in(key, 2), count)]


def centred(stream_key, shape, scale, reach, pieces=(), kind=jnp.bfloat16):
    loudness = shard_levels(stream_key, shape, pieces, -0.22, 0.18) if pieces else 1.0
    values = jax.random.normal(stream_key, shape, jnp.float32) * scale * loudness
    return jnp.minimum(jnp.maximum(values, -reach), reach).astype(kind)


def setup_inputs(seed: int = 0) -> dict:
    splits = jax.random.split(jax.random.key(seed), 17)
    residual = centred(splits[0], (TOKENS, D), 0.05, 0.29882812, ((0, 64), (1, 4)))
    query = draw_query(jax.random.fold_in(splits[16], 71), 0)
    new_keys = centred(splits[2], (TOKENS, HEADS * HD), 1.0, 6.0, ((0, 64), (1, 4)))
    new_values = centred(splits[3], (TOKENS, HEADS * HD), 1.0, 6.0, ((0, 64), (1, 4)))
    leaf_kv = centred(splits[4], (2, REQS * LEAF, HEADS * HD), 1.0, 6.0, ((1, 64), (2, 4)))
    branch_kv = centred(splits[5], (2, BRANCHES * BR, HEADS * HD), 1.0, 6.0, ((1, 64), (2, 4)))
    root_kv = draw_root_kv(jax.random.fold_in(splits[16], 71), 0)
    out_weight = centred(splits[7], (HEADS * HD, D), (HEADS * HD) ** -0.5, 0.125, ((0, 4),))
    norm_gain = jnp.clip(1.0 + 0.15 * jax.random.normal(splits[8], (D,), jnp.float32), 0.25, 1.75)
    norm_bias = centred(splits[9], (D,), 0.3, 1.8, (), jnp.float32)
    up_weight = centred(splits[10], (D, FF), D ** -0.5, 0.125, ((1, 4),))
    up_bias = centred(splits[11], (FF,), 0.5, 3.0, ((0, 4),), jnp.float32)
    down_weight = centred(splits[12], (FF, D), FF ** -0.5, 0.09375, ((0, 4),))
    down_bias = centred(splits[13], (D,), 0.3, 1.8, (), jnp.float32)
    segment = jnp.searchsorted(jnp.cumsum(ragged_sizes(splits[14], BRANCHES, REQS, SEG_MOST, 2)), jnp.arange(REQS), side="right").astype(jnp.int32)
    new_len = ragged_sizes(splits[15], REQS, TOTAL_NEW, NEW, 2).astype(jnp.int32)
    return dict(residual=residual, query=query, new_keys=new_keys, new_values=new_values, leaf_kv=leaf_kv, branch_kv=branch_kv, root_kv=root_kv, out_weight=out_weight, norm_gain=norm_gain, norm_bias=norm_bias, up_weight=up_weight, up_bias=up_bias, down_weight=down_weight, down_bias=down_bias, segment=segment, new_len=new_len)


NEGATIVE_FILL = -1e+30
NORM_EPSILON = 1e-05

def reference(residual, query, new_keys, new_values, leaf_kv, branch_kv, root_kv, out_weight, norm_gain, norm_bias, up_weight, up_bias, down_weight, down_bias, segment, new_len):
    entries = segment.shape[0]
    positions = jnp.arange(entries, dtype=jnp.int32)
    prefix = ROOT + BR + LEAF
    branch_keys = branch_kv[0].reshape(BR, BRANCHES, HEADS * HD)
    branch_values = branch_kv[1].reshape(BR, BRANCHES, HEADS * HD)

    def one_request(request):
        request = request.astype(jnp.int32)
        row_first = (request * NEW).astype(jnp.int32)
        query_rows = lax.dynamic_slice_in_dim(query, row_first, NEW, 0)
        node = segment[request].astype(jnp.int32)
        leaf_first = (request * LEAF).astype(jnp.int32)
        node_keys = lax.dynamic_index_in_dim(branch_keys, node, 1, keepdims=False)
        node_values = lax.dynamic_index_in_dim(branch_values, node, 1, keepdims=False)
        key_rows = jnp.concatenate([root_kv[0], node_keys, lax.dynamic_slice_in_dim(leaf_kv[0], leaf_first, LEAF, 0), lax.dynamic_slice_in_dim(new_keys, row_first, NEW, 0)], axis=0)
        value_rows = jnp.concatenate([root_kv[1], node_values, lax.dynamic_slice_in_dim(leaf_kv[1], leaf_first, LEAF, 0), lax.dynamic_slice_in_dim(new_values, row_first, NEW, 0)], axis=0)
        query_heads = query_rows.astype(jnp.float32).reshape(NEW, HEADS, HD)
        key_heads = key_rows.astype(jnp.float32).reshape(-1, HEADS, HD)
        value_heads = value_rows.astype(jnp.float32).reshape(-1, HEADS, HD)
        scores = jnp.einsum('qhd,khd->hqk', query_heads, key_heads) * HD ** (-0.5)
        column = jnp.arange(prefix + NEW, dtype=jnp.int32)
        query_pos = jnp.arange(NEW, dtype=jnp.int32)
        key_pos = column - prefix
        allowed = (column[None, :] < prefix) | (key_pos[None, :] <= query_pos[:, None]) & (key_pos[None, :] < new_len[request])
        scores = jnp.where(allowed[None], scores, NEGATIVE_FILL)
        largest = lax.optimization_barrier(jnp.max(scores, axis=2, keepdims=True))
        weights = jnp.where(allowed[None], jnp.exp(scores - largest), 0.0)
        totals = lax.optimization_barrier(jnp.sum(weights, axis=2))
        rounded = weights.astype(jnp.bfloat16).astype(jnp.float32)
        mixed = jnp.einsum('hqk,khd->qhd', rounded, value_heads) / jnp.transpose(totals)[:, :, None]
        attention = mixed.reshape(NEW, HEADS * HD).astype(jnp.bfloat16)
        projected = jnp.dot(attention, out_weight, preferred_element_type=jnp.float32)
        residual_rows = lax.dynamic_slice_in_dim(residual, row_first, NEW, 0)
        mid = (residual_rows.astype(jnp.float32) + projected).astype(jnp.bfloat16)
        wide_mid = mid.astype(jnp.float32)
        row_mean = lax.optimization_barrier(jnp.mean(wide_mid, axis=1, keepdims=True))
        row_var = lax.optimization_barrier(jnp.mean(wide_mid * wide_mid, axis=1, keepdims=True)) - row_mean * row_mean
        normed = ((wide_mid - row_mean) * lax.rsqrt(row_var + NORM_EPSILON) * norm_gain + norm_bias).astype(jnp.bfloat16)
        up_sum = jnp.dot(normed, up_weight, preferred_element_type=jnp.float32) + up_bias
        hidden = jax.nn.gelu(up_sum, approximate=False).astype(jnp.bfloat16)
        down_sum = jnp.dot(hidden, down_weight, preferred_element_type=jnp.float32)
        return (down_sum + down_bias + wide_mid).astype(jnp.bfloat16)
    return lax.map(one_request, positions).reshape(TOKENS, D)
```

```python
import jax
import jax.numpy as jnp
from jax import lax
from jax.sharding import PartitionSpec as P

HD = 128


NEGATIVE_FILL = -1e30
NORM_EPSILON = 1e-05
BLOCK_KEYS = 512


def attend(running, query_heads, key_rows, value_rows, allowed):
    largest, totals, accumulated = running
    head_count = query_heads.shape[1]
    head_width = query_heads.shape[2]
    key_heads = key_rows.reshape(key_rows.shape[0], head_count, head_width)
    value_heads = value_rows.reshape(value_rows.shape[0], head_count, head_width)
    scores = jnp.einsum(
        "qhd,khd->hqk", query_heads, key_heads, preferred_element_type=jnp.float32
    ) * head_width ** (-0.5)
    scores = jnp.where(allowed, scores, NEGATIVE_FILL)
    new_largest = jnp.maximum(largest, jnp.max(scores, axis=2))
    weights = jnp.where(allowed, jnp.exp(scores - new_largest[:, :, None]), 0.0)
    factor = jnp.exp(largest - new_largest)
    accumulated = accumulated * factor[:, :, None] + jnp.einsum(
        "hqk,khd->hqd",
        weights.astype(jnp.bfloat16),
        value_heads,
        preferred_element_type=jnp.float32,
    )
    totals = totals * factor + jnp.sum(weights, axis=2)
    return (new_largest, totals, accumulated)


def attend_blocks(running, query_heads, key_rows, value_rows):
    for block_start in range(0, key_rows.shape[0], BLOCK_KEYS):
        running = attend(
            running,
            query_heads,
            key_rows[block_start : block_start + BLOCK_KEYS],
            value_rows[block_start : block_start + BLOCK_KEYS],
            True,
        )
    return running


def per_device(
    residual,
    query,
    new_keys,
    new_values,
    leaf_kv,
    branch_kv,
    root_kv,
    out_weight,
    norm_gain,
    norm_bias,
    up_weight,
    up_bias,
    down_weight,
    down_bias,
    segment,
    new_len,
):
    row_count = query.shape[0]
    head_count = query.shape[1] // HD
    query_heads = query.reshape(row_count, head_count, HD)
    device = lax.axis_index("seq")
    seq_size = lax.axis_size("seq")
    branch_count = seq_size // 4
    feature_width = branch_kv.shape[2]

    root_full = lax.all_gather(root_kv, "seq", axis=1, tiled=True)

    local_rows = branch_kv.shape[1] // branch_count
    branch_local = branch_kv.reshape(2, local_rows, branch_count, feature_width)
    picked = jnp.take(branch_local, segment, axis=2)
    picked = jnp.transpose(picked, (2, 0, 1, 3))
    arrived = lax.all_to_all(picked, "seq", 0, 0, tiled=True)
    branch_mine = jnp.transpose(arrived, (1, 0, 2, 3)).reshape(
        2, seq_size * local_rows, feature_width
    )

    running = (
        jnp.full((head_count, row_count), NEGATIVE_FILL, jnp.float32),
        jnp.zeros((head_count, row_count), jnp.float32),
        jnp.zeros((head_count, row_count, HD), jnp.float32),
    )
    query_pos = jnp.arange(row_count, dtype=jnp.int32)
    allowed_new = (query_pos[None, :] <= query_pos[:, None]) & (
        query_pos[None, :] < new_len[device]
    )
    running = attend(running, query_heads, new_keys, new_values, allowed_new[None])
    running = attend(running, query_heads, leaf_kv[0], leaf_kv[1], True)
    running = attend_blocks(running, query_heads, branch_mine[0], branch_mine[1])
    running = attend_blocks(running, query_heads, root_full[0], root_full[1])
    largest, totals, accumulated = running
    attention = (
        jnp.transpose(accumulated / totals[:, :, None], (1, 0, 2))
        .reshape(row_count, head_count * HD)
        .astype(jnp.bfloat16)
    )
    projected = jnp.dot(attention, out_weight, preferred_element_type=jnp.float32)
    share_width = residual.shape[1]
    column = lax.axis_index("tensor") * share_width
    own_residual = lax.dynamic_update_slice_in_dim(
        jnp.zeros(projected.shape, jnp.float32), residual.astype(jnp.float32), column, 1
    )
    mid_full = lax.psum((projected + own_residual).astype(jnp.bfloat16), "tensor")
    wide_mid = mid_full.astype(jnp.float32)
    row_mean = jnp.mean(wide_mid, axis=1, keepdims=True)
    row_var = jnp.mean(wide_mid * wide_mid, axis=1, keepdims=True) - row_mean * row_mean
    normed = (
        (wide_mid - row_mean) * lax.rsqrt(row_var + NORM_EPSILON) * norm_gain + norm_bias
    ).astype(jnp.bfloat16)
    up_sum = jnp.dot(normed, up_weight, preferred_element_type=jnp.float32)
    mid_share = lax.dynamic_slice_in_dim(mid_full, column, share_width, 1)
    hidden = jax.nn.gelu(up_sum + up_bias, approximate=False).astype(jnp.bfloat16)
    partial_value = jnp.dot(hidden, down_weight, preferred_element_type=jnp.float32)
    summed = lax.psum_scatter(
        partial_value.astype(jnp.bfloat16), "tensor", scatter_dimension=1, tiled=True
    ).astype(jnp.float32)
    down_share = lax.dynamic_slice_in_dim(down_bias, column, share_width, 0)
    return (summed + down_share + mid_share.astype(jnp.float32)).astype(jnp.bfloat16)


def solution(mesh):
    return jax.shard_map(
        per_device,
        mesh=mesh,
        in_specs=(
            P("seq", "tensor"),
            P("seq", "tensor"),
            P("seq", "tensor"),
            P("seq", "tensor"),
            P(None, "seq", "tensor"),
            P(None, "seq", "tensor"),
            P(None, "seq", "tensor"),
            P("tensor", None),
            P(),
            P(),
            P(None, "tensor"),
            P("tensor"),
            P("tensor", None),
            P(),
            P(),
            P(),
        ),
        out_specs=P("seq", "tensor"),
        check_vma=False,
    )
```

```python
import jax
import jax.numpy as jnp
from jax import lax
from jax.sharding import PartitionSpec as P

HD = 128


NEGATIVE_FILL = -1e30
NORM_EPSILON = 1e-05
BLOCK_KEYS = 512


def attend(running, query_heads, key_heads, value_heads, allowed):
    largest, totals, accumulated = running
    head_width = query_heads.shape[2]
    scores = jnp.einsum(
        "hqd,hkd->hqk", query_heads, key_heads, preferred_element_type=jnp.float32
    ) * head_width ** (-0.5)
    scores = jnp.where(allowed, scores, NEGATIVE_FILL)
    new_largest = jnp.maximum(largest, jnp.max(scores, axis=2))
    weights = jnp.where(allowed, jnp.exp(scores - new_largest[:, :, None]), 0.0)
    factor = jnp.exp(largest - new_largest)
    accumulated = accumulated * factor[:, :, None] + jnp.einsum(
        "hqk,hkd->hqd",
        weights.astype(jnp.bfloat16),
        value_heads,
        preferred_element_type=jnp.float32,
    )
    totals = totals * factor + jnp.sum(weights, axis=2)
    return (new_largest, totals, accumulated)


def attend_blocks(running, query_heads, key_heads, value_heads):
    for block_start in range(0, key_heads.shape[1], BLOCK_KEYS):
        running = attend(
            running,
            query_heads,
            key_heads[:, block_start : block_start + BLOCK_KEYS],
            value_heads[:, block_start : block_start + BLOCK_KEYS],
            True,
        )
    return running


def head_major(rows, head_count):
    lead = rows.shape[:-2]
    split = rows.reshape(lead + (rows.shape[-2], head_count, HD))
    order = tuple(range(len(lead))) + (len(lead) + 1, len(lead), len(lead) + 2)
    return jnp.transpose(split, order)


def tensor_sum_scatter(partial, parts):
    rows, width = partial.shape
    pieces = jnp.transpose(
        partial.astype(jnp.bfloat16).reshape(rows, parts, width // parts), (1, 0, 2)
    )
    arrived = lax.all_to_all(pieces, "tensor", 0, 0, tiled=True)
    return jnp.sum(arrived.astype(jnp.float32), axis=0)


def tensor_gather(share, parts):
    rows, width = share.shape
    copies = jnp.broadcast_to(share[None], (parts, rows, width))
    arrived = lax.all_to_all(copies, "tensor", 0, 0, tiled=True)
    return jnp.transpose(arrived, (1, 0, 2)).reshape(rows, parts * width)


def per_device(
    residual,
    query,
    new_keys,
    new_values,
    leaf_kv,
    branch_kv,
    root_kv,
    out_weight,
    norm_gain,
    norm_bias,
    up_weight,
    up_bias,
    down_weight,
    down_bias,
    segment,
    new_len,
):
    row_count = query.shape[0]
    head_count = query.shape[1] // HD
    query_heads = head_major(query, head_count)
    device = lax.axis_index("seq")
    seq_size = lax.axis_size("seq")
    parts = lax.axis_size("tensor")
    branch_count = seq_size // 4
    feature_width = branch_kv.shape[2]

    root_full = lax.all_gather(head_major(root_kv, head_count), "seq", axis=2, tiled=True)

    local_rows = branch_kv.shape[1] // branch_count
    branch_local = branch_kv.reshape(2, local_rows, branch_count, feature_width)
    picked = jnp.take(branch_local, segment, axis=2)
    picked = head_major(jnp.transpose(picked, (2, 0, 1, 3)), head_count)
    arrived = lax.all_to_all(picked, "seq", 0, 0, tiled=True)
    branch_mine = jnp.transpose(arrived, (1, 2, 0, 3, 4)).reshape(
        2, head_count, seq_size * local_rows, HD
    )

    running = (
        jnp.full((head_count, row_count), NEGATIVE_FILL, jnp.float32),
        jnp.zeros((head_count, row_count), jnp.float32),
        jnp.zeros((head_count, row_count, HD), jnp.float32),
    )
    query_pos = jnp.arange(row_count, dtype=jnp.int32)
    allowed_new = (query_pos[None, :] <= query_pos[:, None]) & (
        query_pos[None, :] < new_len[device]
    )
    running = attend(
        running,
        query_heads,
        head_major(new_keys, head_count),
        head_major(new_values, head_count),
        allowed_new[None],
    )
    leaf_heads = head_major(leaf_kv, head_count)
    running = attend(running, query_heads, leaf_heads[0], leaf_heads[1], True)
    running = attend_blocks(running, query_heads, branch_mine[0], branch_mine[1])
    running = attend_blocks(running, query_heads, root_full[0], root_full[1])
    largest, totals, accumulated = running
    attention = (
        jnp.transpose(accumulated / totals[:, :, None], (1, 0, 2))
        .reshape(row_count, head_count * HD)
        .astype(jnp.bfloat16)
    )
    projected = jnp.dot(attention, out_weight, preferred_element_type=jnp.float32)
    share_width = residual.shape[1]
    column = lax.axis_index("tensor") * share_width
    mid_share = (
        tensor_sum_scatter(projected, parts) + residual.astype(jnp.float32)
    ).astype(jnp.bfloat16)
    mid_full = tensor_gather(mid_share, parts)
    wide_mid = mid_full.astype(jnp.float32)
    row_mean = jnp.mean(wide_mid, axis=1, keepdims=True)
    row_var = jnp.mean(wide_mid * wide_mid, axis=1, keepdims=True) - row_mean * row_mean
    normed = (
        (wide_mid - row_mean) * lax.rsqrt(row_var + NORM_EPSILON) * norm_gain + norm_bias
    ).astype(jnp.bfloat16)
    up_sum = jnp.dot(normed, up_weight, preferred_element_type=jnp.float32)
    hidden = jax.nn.gelu(up_sum + up_bias, approximate=False).astype(jnp.bfloat16)
    partial_value = jnp.dot(hidden, down_weight, preferred_element_type=jnp.float32)
    summed = tensor_sum_scatter(partial_value, parts)
    down_share = lax.dynamic_slice_in_dim(down_bias, column, share_width, 0)
    return (summed + down_share + mid_share.astype(jnp.float32)).astype(jnp.bfloat16)


def solution(mesh):
    return jax.shard_map(
        per_device,
        mesh=mesh,
        in_specs=(
            P("seq", "tensor"),
            P("seq", "tensor"),
            P("seq", "tensor"),
            P("seq", "tensor"),
            P(None, "seq", "tensor"),
            P(None, "seq", "tensor"),
            P(None, "seq", "tensor"),
            P("tensor", None),
            P(),
            P(),
            P(None, "tensor"),
            P("tensor"),
            P("tensor", None),
            P(),
            P(),
            P(),
        ),
        out_specs=P("seq", "tensor"),
        check_vma=False,
    )
```

```python
import jax
import jax.numpy as jnp
from jax import lax
from jax.sharding import PartitionSpec as P

HD = 128


NEGATIVE_FILL = -1e30
NORM_EPSILON = 1e-05
BLOCK_KEYS = 512


def attend(running, query_heads, key_heads, value_heads, allowed):
    largest, totals, accumulated = running
    head_width = query_heads.shape[2]
    scores = jnp.einsum(
        "hqd,hkd->hqk", query_heads, key_heads, preferred_element_type=jnp.float32
    ) * head_width ** (-0.5)
    scores = jnp.where(allowed, scores, NEGATIVE_FILL)
    new_largest = jnp.maximum(largest, jnp.max(scores, axis=2))
    weights = jnp.where(allowed, jnp.exp(scores - new_largest[:, :, None]), 0.0)
    factor = jnp.exp(largest - new_largest)
    accumulated = accumulated * factor[:, :, None] + jnp.einsum(
        "hqk,hkd->hqd",
        weights.astype(jnp.bfloat16),
        value_heads,
        preferred_element_type=jnp.float32,
    )
    totals = totals * factor + jnp.sum(weights, axis=2)
    return (new_largest, totals, accumulated)


def attend_blocks(running, query_heads, key_heads, value_heads):
    for block_start in range(0, key_heads.shape[1], BLOCK_KEYS):
        running = attend(
            running,
            query_heads,
            key_heads[:, block_start : block_start + BLOCK_KEYS],
            value_heads[:, block_start : block_start + BLOCK_KEYS],
            True,
        )
    return running


def head_major(rows, head_count):
    lead = rows.shape[:-2]
    split = rows.reshape(lead + (rows.shape[-2], head_count, HD))
    order = tuple(range(len(lead))) + (len(lead) + 1, len(lead), len(lead) + 2)
    return jnp.transpose(split, order)


def tensor_sum_scatter(partial, parts):
    rows, width = partial.shape
    pieces = jnp.transpose(
        partial.astype(jnp.bfloat16).reshape(rows, parts, width // parts), (1, 0, 2)
    )
    arrived = lax.all_to_all(pieces, "tensor", 0, 0, tiled=True)
    return jnp.sum(arrived.astype(jnp.float32), axis=0)


def tensor_gather(share, parts):
    rows, width = share.shape
    copies = jnp.broadcast_to(share[None], (parts, rows, width))
    arrived = lax.all_to_all(copies, "tensor", 0, 0, tiled=True)
    return jnp.transpose(arrived, (1, 0, 2)).reshape(rows, parts * width)


def shift_pairs(shape, axis, step):
    pairs = []
    for index in range(shape[0] * shape[1] * shape[2]):
        place = [index // (shape[1] * shape[2]), (index // shape[2]) % shape[1], index % shape[2]]
        place[axis] = (place[axis] + step) % shape[axis]
        pairs.append((index, (place[0] * shape[1] + place[1]) * shape[2] + place[2]))
    return pairs


def ring_along(block, shape, axis):
    size = shape[axis]
    up = shift_pairs(shape, axis, 1)
    down = shift_pairs(shape, axis, -1)
    pieces = [block]
    from_below = block
    from_above = block
    for _ in range((size - 1) // 2):
        from_below = lax.ppermute(from_below, "seq", up)
        from_above = lax.ppermute(from_above, "seq", down)
        pieces += [from_below, from_above]
    if size % 2 == 0:
        half = block.shape[2] // 2
        first = lax.ppermute(from_below[:, :, :half], "seq", up)
        second = lax.ppermute(from_above[:, :, half:], "seq", down)
        pieces += [first, second]
    return jnp.concatenate(pieces, axis=2)


def ring_gather_seq(block, seq_size):
    cores = 2
    lanes = 4
    shape = (seq_size // (lanes * cores), lanes, cores)
    gathered = ring_along(block, shape, 0)
    gathered = ring_along(gathered, shape, 1)
    partner = lax.ppermute(gathered, "seq", shift_pairs(shape, 2, 1))
    return jnp.concatenate([gathered, partner], axis=2)


def per_device(
    residual,
    query,
    new_keys,
    new_values,
    leaf_kv,
    branch_kv,
    root_kv,
    out_weight,
    norm_gain,
    norm_bias,
    up_weight,
    up_bias,
    down_weight,
    down_bias,
    segment,
    new_len,
):
    row_count = query.shape[0]
    head_count = query.shape[1] // HD
    query_heads = head_major(query, head_count)
    device = lax.axis_index("seq")
    seq_size = lax.axis_size("seq")
    parts = lax.axis_size("tensor")
    branch_count = seq_size // 4
    feature_width = branch_kv.shape[2]

    root_full = ring_gather_seq(head_major(root_kv, head_count), seq_size)

    local_rows = branch_kv.shape[1] // branch_count
    branch_local = branch_kv.reshape(2, local_rows, branch_count, feature_width)
    picked = jnp.take(branch_local, segment, axis=2)
    picked = head_major(jnp.transpose(picked, (2, 0, 1, 3)), head_count)
    arrived = lax.all_to_all(picked, "seq", 0, 0, tiled=True)
    branch_mine = jnp.transpose(arrived, (1, 2, 0, 3, 4)).reshape(
        2, head_count, seq_size * local_rows, HD
    )

    running = (
        jnp.full((head_count, row_count), NEGATIVE_FILL, jnp.float32),
        jnp.zeros((head_count, row_count), jnp.float32),
        jnp.zeros((head_count, row_count, HD), jnp.float32),
    )
    query_pos = jnp.arange(row_count, dtype=jnp.int32)
    allowed_new = (query_pos[None, :] <= query_pos[:, None]) & (
        query_pos[None, :] < new_len[device]
    )
    running = attend(
        running,
        query_heads,
        head_major(new_keys, head_count),
        head_major(new_values, head_count),
        allowed_new[None],
    )
    leaf_heads = head_major(leaf_kv, head_count)
    running = attend(running, query_heads, leaf_heads[0], leaf_heads[1], True)
    running = attend_blocks(running, query_heads, branch_mine[0], branch_mine[1])
    running = attend_blocks(running, query_heads, root_full[0], root_full[1])
    largest, totals, accumulated = running
    attention = (
        jnp.transpose(accumulated / totals[:, :, None], (1, 0, 2))
        .reshape(row_count, head_count * HD)
        .astype(jnp.bfloat16)
    )
    projected = jnp.dot(attention, out_weight, preferred_element_type=jnp.float32)
    share_width = residual.shape[1]
    column = lax.axis_index("tensor") * share_width
    mid_share = (
        tensor_sum_scatter(projected, parts) + residual.astype(jnp.float32)
    ).astype(jnp.bfloat16)
    mid_full = tensor_gather(mid_share, parts)
    wide_mid = mid_full.astype(jnp.float32)
    row_mean = jnp.mean(wide_mid, axis=1, keepdims=True)
    row_var = jnp.mean(wide_mid * wide_mid, axis=1, keepdims=True) - row_mean * row_mean
    normed = (
        (wide_mid - row_mean) * lax.rsqrt(row_var + NORM_EPSILON) * norm_gain + norm_bias
    ).astype(jnp.bfloat16)
    up_sum = jnp.dot(normed, up_weight, preferred_element_type=jnp.float32)
    hidden = lax.optimization_barrier(
        jax.nn.gelu(up_sum + up_bias, approximate=False).astype(jnp.bfloat16)
    )
    partial_value = jnp.dot(hidden, down_weight, preferred_element_type=jnp.float32)
    summed = tensor_sum_scatter(partial_value, parts)
    down_share = lax.dynamic_slice_in_dim(down_bias, column, share_width, 0)
    return (summed + down_share + mid_share.astype(jnp.float32)).astype(jnp.bfloat16)


def solution(mesh):
    return jax.shard_map(
        per_device,
        mesh=mesh,
        in_specs=(
            P("seq", "tensor"),
            P("seq", "tensor"),
            P("seq", "tensor"),
            P("seq", "tensor"),
            P(None, "seq", "tensor"),
            P(None, "seq", "tensor"),
            P(None, "seq", "tensor"),
            P("tensor", None),
            P(),
            P(),
            P(None, "tensor"),
            P("tensor"),
            P("tensor", None),
            P(),
            P(),
            P(),
        ),
        out_specs=P("seq", "tensor"),
        check_vma=False,
    )
```

```python
import jax
import jax.numpy as jnp
from jax import lax
from jax.sharding import PartitionSpec as P

HD = 128


NEGATIVE_FILL = -1e30
NORM_EPSILON = 1e-05
BLOCK_KEYS = 512


def attend(running, query_heads, key_heads, value_heads, allowed):
    largest, totals, accumulated = running
    head_width = query_heads.shape[2]
    scores = jnp.einsum(
        "hqd,hkd->hqk", query_heads, key_heads, preferred_element_type=jnp.float32
    ) * head_width ** (-0.5)
    scores = jnp.where(allowed, scores, NEGATIVE_FILL)
    new_largest = jnp.maximum(largest, jnp.max(scores, axis=2))
    weights = jnp.where(allowed, jnp.exp(scores - new_largest[:, :, None]), 0.0)
    factor = jnp.exp(largest - new_largest)
    accumulated = accumulated * factor[:, :, None] + jnp.einsum(
        "hqk,hkd->hqd",
        weights.astype(jnp.bfloat16),
        value_heads,
        preferred_element_type=jnp.float32,
    )
    totals = totals * factor + jnp.sum(weights, axis=2)
    return (new_largest, totals, accumulated)


def attend_blocks(running, query_heads, key_heads, value_heads):
    for block_start in range(0, key_heads.shape[1], BLOCK_KEYS):
        running = attend(
            running,
            query_heads,
            key_heads[:, block_start : block_start + BLOCK_KEYS],
            value_heads[:, block_start : block_start + BLOCK_KEYS],
            True,
        )
    return running


def head_major(rows, head_count):
    lead = rows.shape[:-2]
    split = rows.reshape(lead + (rows.shape[-2], head_count, HD))
    order = tuple(range(len(lead))) + (len(lead) + 1, len(lead), len(lead) + 2)
    return jnp.transpose(split, order)


def tensor_sum_scatter(partial, parts):
    rows, width = partial.shape
    pieces = jnp.transpose(
        partial.astype(jnp.bfloat16).reshape(rows, parts, width // parts), (1, 0, 2)
    )
    arrived = lax.all_to_all(pieces, "tensor", 0, 0, tiled=True)
    return jnp.sum(arrived.astype(jnp.float32), axis=0)


def tensor_gather(share, parts):
    rows, width = share.shape
    copies = jnp.broadcast_to(share[None], (parts, rows, width))
    arrived = lax.all_to_all(copies, "tensor", 0, 0, tiled=True)
    return jnp.transpose(arrived, (1, 0, 2)).reshape(rows, parts * width)


def shift_pairs(shape, axis, step):
    pairs = []
    for index in range(shape[0] * shape[1] * shape[2]):
        place = [index // (shape[1] * shape[2]), (index // shape[2]) % shape[1], index % shape[2]]
        place[axis] = (place[axis] + step) % shape[axis]
        pairs.append((index, (place[0] * shape[1] + place[1]) * shape[2] + place[2]))
    return pairs


def ring_along(block, shape, axis):
    size = shape[axis]
    up = shift_pairs(shape, axis, 1)
    down = shift_pairs(shape, axis, -1)
    pieces = [block]
    from_below = block
    from_above = block
    for _ in range((size - 1) // 2):
        from_below = lax.ppermute(from_below, "seq", up)
        from_above = lax.ppermute(from_above, "seq", down)
        pieces += [from_below, from_above]
    if size % 2 == 0:
        half = block.shape[2] // 2
        first = lax.ppermute(from_below[:, :, :half], "seq", up)
        second = lax.ppermute(from_above[:, :, half:], "seq", down)
        pieces += [first, second]
    return jnp.concatenate(pieces, axis=2)


def ring_gather_seq(block, seq_size, companion):
    cores = 2
    lanes = 4
    shape = (seq_size // (lanes * cores), lanes, cores)
    gathered = ring_along(block, shape, 0)
    gathered = ring_along(gathered, shape, 1)
    gathered, companion = lax.optimization_barrier((gathered, companion))
    partner = lax.ppermute(gathered, "seq", shift_pairs(shape, 2, 1))
    return jnp.concatenate([gathered, partner], axis=2), companion


def per_device(
    residual,
    query,
    new_keys,
    new_values,
    leaf_kv,
    branch_kv,
    root_kv,
    out_weight,
    norm_gain,
    norm_bias,
    up_weight,
    up_bias,
    down_weight,
    down_bias,
    segment,
    new_len,
):
    row_count = query.shape[0]
    head_count = query.shape[1] // HD
    query_heads = head_major(query, head_count)
    device = lax.axis_index("seq")
    seq_size = lax.axis_size("seq")
    parts = lax.axis_size("tensor")
    branch_count = seq_size // 4
    feature_width = branch_kv.shape[2]

    local_rows = branch_kv.shape[1] // branch_count
    branch_local = branch_kv.reshape(2, local_rows, branch_count, feature_width)
    picked = jnp.take(branch_local, segment, axis=2)
    picked = head_major(jnp.transpose(picked, (2, 0, 1, 3)), head_count)
    arrived = lax.all_to_all(picked, "seq", 0, 0, tiled=True)

    root_full, arrived = ring_gather_seq(head_major(root_kv, head_count), seq_size, arrived)
    branch_mine = jnp.transpose(arrived, (1, 2, 0, 3, 4)).reshape(
        2, head_count, seq_size * local_rows, HD
    )

    running = (
        jnp.full((head_count, row_count), NEGATIVE_FILL, jnp.float32),
        jnp.zeros((head_count, row_count), jnp.float32),
        jnp.zeros((head_count, row_count, HD), jnp.float32),
    )
    query_pos = jnp.arange(row_count, dtype=jnp.int32)
    allowed_new = (query_pos[None, :] <= query_pos[:, None]) & (
        query_pos[None, :] < new_len[device]
    )
    running = attend(
        running,
        query_heads,
        head_major(new_keys, head_count),
        head_major(new_values, head_count),
        allowed_new[None],
    )
    leaf_heads = head_major(leaf_kv, head_count)
    running = attend(running, query_heads, leaf_heads[0], leaf_heads[1], True)
    running = attend_blocks(running, query_heads, branch_mine[0], branch_mine[1])
    running = attend_blocks(running, query_heads, root_full[0], root_full[1])
    largest, totals, accumulated = running
    attention = (
        jnp.transpose(accumulated / totals[:, :, None], (1, 0, 2))
        .reshape(row_count, head_count * HD)
        .astype(jnp.bfloat16)
    )
    projected = jnp.dot(attention, out_weight, preferred_element_type=jnp.float32)
    share_width = residual.shape[1]
    column = lax.axis_index("tensor") * share_width
    mid_share = (
        tensor_sum_scatter(projected, parts) + residual.astype(jnp.float32)
    ).astype(jnp.bfloat16)
    mid_full = tensor_gather(mid_share, parts)
    wide_mid = mid_full.astype(jnp.float32)
    row_mean = jnp.mean(wide_mid, axis=1, keepdims=True)
    row_var = jnp.mean(wide_mid * wide_mid, axis=1, keepdims=True) - row_mean * row_mean
    normed = (
        (wide_mid - row_mean) * lax.rsqrt(row_var + NORM_EPSILON) * norm_gain + norm_bias
    ).astype(jnp.bfloat16)
    up_sum = jnp.dot(normed, up_weight, preferred_element_type=jnp.float32)
    hidden = lax.optimization_barrier(
        jax.nn.gelu(up_sum + up_bias, approximate=False).astype(jnp.bfloat16)
    )
    partial_value = jnp.dot(hidden, down_weight, preferred_element_type=jnp.float32)
    summed = tensor_sum_scatter(partial_value, parts)
    down_share = lax.dynamic_slice_in_dim(down_bias, column, share_width, 0)
    return (summed + down_share + mid_share.astype(jnp.float32)).astype(jnp.bfloat16)


def solution(mesh):
    return jax.shard_map(
        per_device,
        mesh=mesh,
        in_specs=(
            P("seq", "tensor"),
            P("seq", "tensor"),
            P("seq", "tensor"),
            P("seq", "tensor"),
            P(None, "seq", "tensor"),
            P(None, "seq", "tensor"),
            P(None, "seq", "tensor"),
            P("tensor", None),
            P(),
            P(),
            P(None, "tensor"),
            P("tensor"),
            P("tensor", None),
            P(),
            P(),
            P(),
        ),
        out_specs=P("seq", "tensor"),
        check_vma=False,
    )
```

```python
import jax
import jax.numpy as jnp
from jax import lax
from jax.sharding import PartitionSpec as P

HD = 128


NEGATIVE_FILL = -1e30
NORM_EPSILON = 1e-05
BLOCK_KEYS = 512


def attend(running, query_heads, key_heads, value_heads, allowed):
    largest, totals, accumulated = running
    head_width = query_heads.shape[2]
    scores = jnp.einsum(
        "hqd,hkd->hqk", query_heads, key_heads, preferred_element_type=jnp.float32
    ) * head_width ** (-0.5)
    scores = jnp.where(allowed, scores, NEGATIVE_FILL)
    new_largest = jnp.maximum(largest, jnp.max(scores, axis=2))
    weights = jnp.where(allowed, jnp.exp(scores - new_largest[:, :, None]), 0.0)
    factor = jnp.exp(largest - new_largest)
    accumulated = accumulated * factor[:, :, None] + jnp.einsum(
        "hqk,hkd->hqd",
        weights.astype(jnp.bfloat16),
        value_heads,
        preferred_element_type=jnp.float32,
    )
    totals = totals * factor + jnp.sum(weights, axis=2)
    return (new_largest, totals, accumulated)


def attend_blocks(running, query_heads, key_heads, value_heads):
    for block_start in range(0, key_heads.shape[1], BLOCK_KEYS):
        running = attend(
            running,
            query_heads,
            key_heads[:, block_start : block_start + BLOCK_KEYS],
            value_heads[:, block_start : block_start + BLOCK_KEYS],
            True,
        )
    return running


def head_major(rows, head_count):
    lead = rows.shape[:-2]
    split = rows.reshape(lead + (rows.shape[-2], head_count, HD))
    order = tuple(range(len(lead))) + (len(lead) + 1, len(lead), len(lead) + 2)
    return jnp.transpose(split, order)


def tensor_sum_scatter(partial, parts):
    rows, width = partial.shape
    pieces = jnp.transpose(
        partial.astype(jnp.bfloat16).reshape(rows, parts, width // parts), (1, 0, 2)
    )
    arrived = lax.all_to_all(pieces, "tensor", 0, 0, tiled=True)
    return jnp.sum(arrived.astype(jnp.float32), axis=0)


def tensor_gather(share, parts):
    rows, width = share.shape
    copies = jnp.broadcast_to(share[None], (parts, rows, width))
    arrived = lax.all_to_all(copies, "tensor", 0, 0, tiled=True)
    return jnp.transpose(arrived, (1, 0, 2)).reshape(rows, parts * width)


def shift_pairs(shape, axis, step):
    pairs = []
    for index in range(shape[0] * shape[1] * shape[2]):
        place = [index // (shape[1] * shape[2]), (index // shape[2]) % shape[1], index % shape[2]]
        place[axis] = (place[axis] + step) % shape[axis]
        pairs.append((index, (place[0] * shape[1] + place[1]) * shape[2] + place[2]))
    return pairs


def ring_along(block, shape, axis):
    size = shape[axis]
    up = shift_pairs(shape, axis, 1)
    down = shift_pairs(shape, axis, -1)
    pieces = [block]
    from_below = block
    from_above = block
    for _ in range((size - 1) // 2):
        from_below = lax.ppermute(from_below, "seq", up)
        from_above = lax.ppermute(from_above, "seq", down)
        pieces += [from_below, from_above]
    if size % 2 == 0:
        half = block.shape[2] // 2
        first = lax.ppermute(from_below[:, :, :half], "seq", up)
        second = lax.ppermute(from_above[:, :, half:], "seq", down)
        pieces += [first, second]
    return pieces


def per_device(
    residual,
    query,
    new_keys,
    new_values,
    leaf_kv,
    branch_kv,
    root_kv,
    out_weight,
    norm_gain,
    norm_bias,
    up_weight,
    up_bias,
    down_weight,
    down_bias,
    segment,
    new_len,
):
    row_count = query.shape[0]
    head_count = query.shape[1] // HD
    query_heads = head_major(query, head_count)
    device = lax.axis_index("seq")
    seq_size = lax.axis_size("seq")
    parts = lax.axis_size("tensor")
    branch_count = seq_size // 4
    feature_width = branch_kv.shape[2]

    cores = 2
    lanes = 4
    ring_shape = (seq_size // (lanes * cores), lanes, cores)
    z_block = jnp.concatenate(ring_along(head_major(root_kv, head_count), ring_shape, 0), axis=2)

    local_rows = branch_kv.shape[1] // branch_count
    branch_local = branch_kv.reshape(2, local_rows, branch_count, feature_width)
    picked = jnp.take(branch_local, segment, axis=2)
    picked = head_major(jnp.transpose(picked, (2, 0, 1, 3)), head_count)
    z_block, picked = lax.optimization_barrier((z_block, picked))
    arrived = lax.all_to_all(picked, "seq", 0, 0, tiled=True)

    x_pieces = ring_along(z_block, ring_shape, 1)
    x_block = jnp.concatenate(x_pieces, axis=2)
    x_block, arrived = lax.optimization_barrier((x_block, arrived))
    partner = lax.ppermute(x_block, "seq", shift_pairs(ring_shape, 2, 1))
    branch_mine = jnp.transpose(arrived, (1, 2, 0, 3, 4)).reshape(
        2, head_count, seq_size * local_rows, HD
    )

    running = (
        jnp.full((head_count, row_count), NEGATIVE_FILL, jnp.float32),
        jnp.zeros((head_count, row_count), jnp.float32),
        jnp.zeros((head_count, row_count, HD), jnp.float32),
    )
    query_pos = jnp.arange(row_count, dtype=jnp.int32)
    allowed_new = (query_pos[None, :] <= query_pos[:, None]) & (
        query_pos[None, :] < new_len[device]
    )
    running = attend(
        running,
        query_heads,
        head_major(new_keys, head_count),
        head_major(new_values, head_count),
        allowed_new[None],
    )
    leaf_heads = head_major(leaf_kv, head_count)
    running = attend(running, query_heads, leaf_heads[0], leaf_heads[1], True)
    for piece in x_pieces:
        running = attend_blocks(running, query_heads, piece[0], piece[1])
    running = attend_blocks(running, query_heads, branch_mine[0], branch_mine[1])
    running = attend_blocks(running, query_heads, partner[0], partner[1])
    largest, totals, accumulated = running
    attention = (
        jnp.transpose(accumulated / totals[:, :, None], (1, 0, 2))
        .reshape(row_count, head_count * HD)
        .astype(jnp.bfloat16)
    )
    projected = jnp.dot(attention, out_weight, preferred_element_type=jnp.float32)
    share_width = residual.shape[1]
    column = lax.axis_index("tensor") * share_width
    mid_share = (
        tensor_sum_scatter(projected, parts) + residual.astype(jnp.float32)
    ).astype(jnp.bfloat16)
    mid_full = tensor_gather(mid_share, parts)
    wide_mid = mid_full.astype(jnp.float32)
    row_mean = jnp.mean(wide_mid, axis=1, keepdims=True)
    row_var = jnp.mean(wide_mid * wide_mid, axis=1, keepdims=True) - row_mean * row_mean
    normed = (
        (wide_mid - row_mean) * lax.rsqrt(row_var + NORM_EPSILON) * norm_gain + norm_bias
    ).astype(jnp.bfloat16)
    up_sum = jnp.dot(normed, up_weight, preferred_element_type=jnp.float32)
    hidden = lax.optimization_barrier(
        jax.nn.gelu(up_sum + up_bias, approximate=False).astype(jnp.bfloat16)
    )
    partial_value = jnp.dot(hidden, down_weight, preferred_element_type=jnp.float32)
    summed = tensor_sum_scatter(partial_value, parts)
    down_share = lax.dynamic_slice_in_dim(down_bias, column, share_width, 0)
    return (summed + down_share + mid_share.astype(jnp.float32)).astype(jnp.bfloat16)


def solution(mesh):
    return jax.shard_map(
        per_device,
        mesh=mesh,
        in_specs=(
            P("seq", "tensor"),
            P("seq", "tensor"),
            P("seq", "tensor"),
            P("seq", "tensor"),
            P(None, "seq", "tensor"),
            P(None, "seq", "tensor"),
            P(None, "seq", "tensor"),
            P("tensor", None),
            P(),
            P(),
            P(None, "tensor"),
            P("tensor"),
            P("tensor", None),
            P(),
            P(),
            P(),
        ),
        out_specs=P("seq", "tensor"),
        check_vma=False,
    )
```

```python
import jax
import jax.numpy as jnp
from jax import lax
from jax.sharding import PartitionSpec as P

HD = 128


NEGATIVE_FILL = -1e30
NORM_EPSILON = 1e-05
BLOCK_KEYS = 512


def attend(running, query_heads, key_heads, value_heads, allowed):
    largest, totals, accumulated = running
    head_width = query_heads.shape[2]
    scores = jnp.einsum(
        "hqd,hkd->hqk", query_heads, key_heads, preferred_element_type=jnp.float32
    ) * head_width ** (-0.5)
    scores = jnp.where(allowed, scores, NEGATIVE_FILL)
    new_largest = jnp.maximum(largest, jnp.max(scores, axis=2))
    weights = jnp.where(allowed, jnp.exp(scores - new_largest[:, :, None]), 0.0)
    factor = jnp.exp(largest - new_largest)
    accumulated = accumulated * factor[:, :, None] + jnp.einsum(
        "hqk,hkd->hqd",
        weights.astype(jnp.bfloat16),
        value_heads,
        preferred_element_type=jnp.float32,
    )
    totals = totals * factor + jnp.sum(weights, axis=2)
    return (new_largest, totals, accumulated)


def attend_blocks(running, query_heads, key_heads, value_heads):
    for block_start in range(0, key_heads.shape[1], BLOCK_KEYS):
        running = attend(
            running,
            query_heads,
            key_heads[:, block_start : block_start + BLOCK_KEYS],
            value_heads[:, block_start : block_start + BLOCK_KEYS],
            True,
        )
    return running


def head_major(rows, head_count):
    lead = rows.shape[:-2]
    split = rows.reshape(lead + (rows.shape[-2], head_count, HD))
    order = tuple(range(len(lead))) + (len(lead) + 1, len(lead), len(lead) + 2)
    return jnp.transpose(split, order)


def tensor_sum_scatter(partial, parts):
    rows, width = partial.shape
    pieces = jnp.transpose(
        partial.astype(jnp.bfloat16).reshape(rows, parts, width // parts), (1, 0, 2)
    )
    arrived = lax.all_to_all(pieces, "tensor", 0, 0, tiled=True)
    return jnp.sum(arrived.astype(jnp.float32), axis=0)


def tensor_gather(share, parts):
    rows, width = share.shape
    copies = jnp.broadcast_to(share[None], (parts, rows, width))
    arrived = lax.all_to_all(copies, "tensor", 0, 0, tiled=True)
    return jnp.transpose(arrived, (1, 0, 2)).reshape(rows, parts * width)


def shift_pairs(shape, axis, step):
    pairs = []
    for index in range(shape[0] * shape[1] * shape[2]):
        place = [index // (shape[1] * shape[2]), (index // shape[2]) % shape[1], index % shape[2]]
        place[axis] = (place[axis] + step) % shape[axis]
        pairs.append((index, (place[0] * shape[1] + place[1]) * shape[2] + place[2]))
    return pairs


def ring_along(block, shape, axis):
    size = shape[axis]
    up = shift_pairs(shape, axis, 1)
    down = shift_pairs(shape, axis, -1)
    pieces = [block]
    from_below = block
    from_above = block
    for _ in range((size - 1) // 2):
        from_below = lax.ppermute(from_below, "seq", up)
        from_above = lax.ppermute(from_above, "seq", down)
        pieces += [from_below, from_above]
    if size % 2 == 0:
        half = block.shape[2] // 2
        first = lax.ppermute(from_below[:, :, :half], "seq", up)
        second = lax.ppermute(from_above[:, :, half:], "seq", down)
        pieces += [first, second]
    return jnp.concatenate(pieces, axis=2)


def ring_gather_seq(block, seq_size, companion):
    cores = 2
    lanes = 4
    shape = (seq_size // (lanes * cores), lanes, cores)
    gathered = ring_along(block, shape, 0)
    gathered = ring_along(gathered, shape, 1)
    gathered, companion = lax.optimization_barrier((gathered, companion))
    partner = lax.ppermute(gathered, "seq", shift_pairs(shape, 2, 1))
    return jnp.concatenate([gathered, partner], axis=2), companion


def tensor_shift(parts, step):
    return [(i, (i + step) % parts) for i in range(parts)]


def per_device(
    residual,
    query,
    new_keys,
    new_values,
    leaf_kv,
    branch_kv,
    root_kv,
    out_weight,
    norm_gain,
    norm_bias,
    up_weight,
    up_bias,
    down_weight,
    down_bias,
    segment,
    new_len,
):
    row_count = query.shape[0]
    head_count = query.shape[1] // HD
    query_heads = head_major(query, head_count)
    device = lax.axis_index("seq")
    seq_size = lax.axis_size("seq")
    parts = lax.axis_size("tensor")
    branch_count = seq_size // 4
    feature_width = branch_kv.shape[2]

    local_rows = branch_kv.shape[1] // branch_count
    branch_local = branch_kv.reshape(2, local_rows, branch_count, feature_width)
    picked = jnp.take(branch_local, segment, axis=2)
    picked = head_major(jnp.transpose(picked, (2, 0, 1, 3)), head_count)
    arrived = lax.all_to_all(picked, "seq", 0, 0, tiled=True)

    root_full, arrived = ring_gather_seq(head_major(root_kv, head_count), seq_size, arrived)
    branch_mine = jnp.transpose(arrived, (1, 2, 0, 3, 4)).reshape(
        2, head_count, seq_size * local_rows, HD
    )

    core = device % 2
    half_columns = out_weight.shape[1] // 2
    weight_half = lax.dynamic_slice_in_dim(out_weight, core * half_columns, half_columns, 1)
    weight_mine = jnp.concatenate(
        [weight_half]
        + [lax.ppermute(weight_half, "tensor", tensor_shift(parts, k)) for k in range(1, parts)],
        axis=0,
    )
    weight_other = lax.ppermute(weight_mine, "seq", [(i, i ^ 1) for i in range(seq_size)])
    residual_blocks = jnp.stack(
        [residual]
        + [lax.ppermute(residual, "tensor", tensor_shift(parts, k)) for k in range(1, parts)]
    )
    block_order = (lax.axis_index("tensor") - jnp.arange(parts)) % parts
    residual_full = jnp.concatenate(
        [residual_blocks[block_order[p]] for p in range(parts)], axis=1
    )

    running = (
        jnp.full((head_count, row_count), NEGATIVE_FILL, jnp.float32),
        jnp.zeros((head_count, row_count), jnp.float32),
        jnp.zeros((head_count, row_count, HD), jnp.float32),
    )
    query_pos = jnp.arange(row_count, dtype=jnp.int32)
    allowed_new = (query_pos[None, :] <= query_pos[:, None]) & (
        query_pos[None, :] < new_len[device]
    )
    running = attend(
        running,
        query_heads,
        head_major(new_keys, head_count),
        head_major(new_values, head_count),
        allowed_new[None],
    )
    leaf_heads = head_major(leaf_kv, head_count)
    running = attend(running, query_heads, leaf_heads[0], leaf_heads[1], True)
    running = attend_blocks(running, query_heads, branch_mine[0], branch_mine[1])
    running = attend_blocks(running, query_heads, root_full[0], root_full[1])
    largest, totals, accumulated = running
    attention = (
        jnp.transpose(accumulated / totals[:, :, None], (1, 0, 2))
        .reshape(row_count, head_count * HD)
        .astype(jnp.bfloat16)
    )
    share_width = residual.shape[1]
    column = lax.axis_index("tensor") * share_width
    attention_blocks = [attention] + [
        lax.ppermute(attention, "tensor", tensor_shift(parts, k)) for k in range(1, parts)
    ]
    attention_all = jnp.concatenate(attention_blocks, axis=1)
    mine = jnp.dot(attention_all, weight_mine, preferred_element_type=jnp.float32)
    other = jnp.dot(attention_all, weight_other, preferred_element_type=jnp.float32)
    first_core = core == 0
    projected = jnp.concatenate(
        [jnp.where(first_core, mine, other), jnp.where(first_core, other, mine)], axis=1
    )
    mid_full = (residual_full.astype(jnp.float32) + projected).astype(jnp.bfloat16)
    mid_share = lax.dynamic_slice_in_dim(mid_full, column, share_width, 1)
    wide_mid = mid_full.astype(jnp.float32)
    row_mean = jnp.mean(wide_mid, axis=1, keepdims=True)
    row_var = jnp.mean(wide_mid * wide_mid, axis=1, keepdims=True) - row_mean * row_mean
    normed = (
        (wide_mid - row_mean) * lax.rsqrt(row_var + NORM_EPSILON) * norm_gain + norm_bias
    ).astype(jnp.bfloat16)
    up_sum = jnp.dot(normed, up_weight, preferred_element_type=jnp.float32)
    hidden = lax.optimization_barrier(
        jax.nn.gelu(up_sum + up_bias, approximate=False).astype(jnp.bfloat16)
    )
    partial_value = jnp.dot(hidden, down_weight, preferred_element_type=jnp.float32)
    summed = tensor_sum_scatter(partial_value, parts)
    down_share = lax.dynamic_slice_in_dim(down_bias, column, share_width, 0)
    return (summed + down_share + mid_share.astype(jnp.float32)).astype(jnp.bfloat16)


def solution(mesh):
    return jax.shard_map(
        per_device,
        mesh=mesh,
        in_specs=(
            P("seq", "tensor"),
            P("seq", "tensor"),
            P("seq", "tensor"),
            P("seq", "tensor"),
            P(None, "seq", "tensor"),
            P(None, "seq", "tensor"),
            P(None, "seq", "tensor"),
            P("tensor", None),
            P(),
            P(),
            P(None, "tensor"),
            P("tensor"),
            P("tensor", None),
            P(),
            P(),
            P(),
        ),
        out_specs=P("seq", "tensor"),
        check_vma=False,
    )
```

```python
import jax
import jax.numpy as jnp
from jax import lax
from jax.sharding import PartitionSpec as P

HD = 128


NEGATIVE_FILL = -1e30
NORM_EPSILON = 1e-05
BLOCK_KEYS = 2048


def attend(running, query_heads, key_heads, value_heads, allowed):
    largest, totals, accumulated = running
    head_width = query_heads.shape[2]
    scores = jnp.einsum(
        "hqd,hkd->hqk", query_heads, key_heads, preferred_element_type=jnp.float32
    ) * head_width ** (-0.5)
    scores = jnp.where(allowed, scores, NEGATIVE_FILL)
    new_largest = jnp.maximum(largest, jnp.max(scores, axis=2))
    weights = jnp.where(allowed, jnp.exp(scores - new_largest[:, :, None]), 0.0)
    factor = jnp.exp(largest - new_largest)
    accumulated = accumulated * factor[:, :, None] + jnp.einsum(
        "hqk,hkd->hqd",
        weights.astype(jnp.bfloat16),
        value_heads,
        preferred_element_type=jnp.float32,
    )
    totals = totals * factor + jnp.sum(weights, axis=2)
    return (new_largest, totals, accumulated)


def attend_blocks(running, query_heads, key_heads, value_heads):
    for block_start in range(0, key_heads.shape[1], BLOCK_KEYS):
        running = attend(
            running,
            query_heads,
            key_heads[:, block_start : block_start + BLOCK_KEYS],
            value_heads[:, block_start : block_start + BLOCK_KEYS],
            True,
        )
    return running


def head_major(rows, head_count):
    lead = rows.shape[:-2]
    split = rows.reshape(lead + (rows.shape[-2], head_count, HD))
    order = tuple(range(len(lead))) + (len(lead) + 1, len(lead), len(lead) + 2)
    return jnp.transpose(split, order)


def tensor_sum_scatter(partial, parts):
    rows, width = partial.shape
    pieces = jnp.transpose(
        partial.astype(jnp.bfloat16).reshape(rows, parts, width // parts), (1, 0, 2)
    )
    arrived = lax.all_to_all(pieces, "tensor", 0, 0, tiled=True)
    return jnp.sum(arrived.astype(jnp.float32), axis=0)


def tensor_gather(share, parts):
    rows, width = share.shape
    copies = jnp.broadcast_to(share[None], (parts, rows, width))
    arrived = lax.all_to_all(copies, "tensor", 0, 0, tiled=True)
    return jnp.transpose(arrived, (1, 0, 2)).reshape(rows, parts * width)


def shift_pairs(shape, axis, step):
    pairs = []
    for index in range(shape[0] * shape[1] * shape[2]):
        place = [index // (shape[1] * shape[2]), (index // shape[2]) % shape[1], index % shape[2]]
        place[axis] = (place[axis] + step) % shape[axis]
        pairs.append((index, (place[0] * shape[1] + place[1]) * shape[2] + place[2]))
    return pairs


def ring_along(block, shape, axis):
    size = shape[axis]
    up = shift_pairs(shape, axis, 1)
    down = shift_pairs(shape, axis, -1)
    pieces = [block]
    from_below = block
    from_above = block
    for _ in range((size - 1) // 2):
        from_below = lax.ppermute(from_below, "seq", up)
        from_above = lax.ppermute(from_above, "seq", down)
        pieces += [from_below, from_above]
    if size % 2 == 0:
        half = block.shape[2] // 2
        first = lax.ppermute(from_below[:, :, :half], "seq", up)
        second = lax.ppermute(from_above[:, :, half:], "seq", down)
        pieces += [first, second]
    return jnp.concatenate(pieces, axis=2)


def ring_gather_seq(block, seq_size, companion):
    cores = 2
    lanes = 4
    shape = (seq_size // (lanes * cores), lanes, cores)
    gathered = ring_along(block, shape, 0)
    gathered = ring_along(gathered, shape, 1)
    gathered, companion = lax.optimization_barrier((gathered, companion))
    partner = lax.ppermute(gathered, "seq", shift_pairs(shape, 2, 1))
    return jnp.concatenate([gathered, partner], axis=2), companion


def per_device(
    residual,
    query,
    new_keys,
    new_values,
    leaf_kv,
    branch_kv,
    root_kv,
    out_weight,
    norm_gain,
    norm_bias,
    up_weight,
    up_bias,
    down_weight,
    down_bias,
    segment,
    new_len,
):
    row_count = query.shape[0]
    head_count = query.shape[1] // HD
    query_heads = head_major(query, head_count)
    device = lax.axis_index("seq")
    seq_size = lax.axis_size("seq")
    parts = lax.axis_size("tensor")
    branch_count = seq_size // 4
    feature_width = branch_kv.shape[2]

    local_rows = branch_kv.shape[1] // branch_count
    branch_local = branch_kv.reshape(2, local_rows, branch_count, feature_width)
    picked = jnp.take(branch_local, segment, axis=2)
    picked = head_major(jnp.transpose(picked, (2, 0, 1, 3)), head_count)
    arrived = lax.all_to_all(picked, "seq", 0, 0, tiled=True)

    root_full, arrived = ring_gather_seq(head_major(root_kv, head_count), seq_size, arrived)
    branch_mine = jnp.transpose(arrived, (1, 2, 0, 3, 4)).reshape(
        2, head_count, seq_size * local_rows, HD
    )

    halves = 2
    half_rows = row_count // halves
    outputs = []
    for part in range(halves):
        rows = slice(part * half_rows, (part + 1) * half_rows)
        outputs.append(
            finish_rows(
                part * half_rows,
                query_heads[:, rows],
                residual[rows],
                new_keys,
                new_values,
                leaf_kv,
                branch_mine,
                root_full,
                new_len[device],
                out_weight,
                norm_gain,
                norm_bias,
                up_weight,
                up_bias,
                down_weight,
                down_bias,
            )
        )
    return jnp.concatenate(outputs, axis=0)


def tensor_scatter_rows(partial, parts):
    me = lax.axis_index("tensor")
    width = partial.shape[1] // parts
    pieces = partial.astype(jnp.bfloat16)
    total = lax.dynamic_slice_in_dim(pieces, me * width, width, 1).astype(jnp.float32)
    for step in range(1, parts):
        block = lax.dynamic_slice_in_dim(pieces, ((me + step) % parts) * width, width, 1)
        total = total + lax.ppermute(block, "tensor", tensor_shift(parts, step)).astype(
            jnp.float32
        )
    return total


def tensor_gather_rows(share, parts):
    me = lax.axis_index("tensor")
    blocks = jnp.stack(
        [share] + [lax.ppermute(share, "tensor", tensor_shift(parts, k)) for k in range(1, parts)]
    )
    order = (me - jnp.arange(parts)) % parts
    return jnp.concatenate([blocks[order[p]] for p in range(parts)], axis=1)


def tensor_shift(parts, step):
    return [(i, (i + step) % parts) for i in range(parts)]


def finish_rows(
    first_row,
    query_heads,
    residual,
    new_keys,
    new_values,
    leaf_kv,
    branch_mine,
    root_full,
    valid,
    out_weight,
    norm_gain,
    norm_bias,
    up_weight,
    up_bias,
    down_weight,
    down_bias,
):
    head_count = query_heads.shape[0]
    row_count = query_heads.shape[1]
    parts = lax.axis_size("tensor")
    running = (
        jnp.full((head_count, row_count), NEGATIVE_FILL, jnp.float32),
        jnp.zeros((head_count, row_count), jnp.float32),
        jnp.zeros((head_count, row_count, HD), jnp.float32),
    )
    query_pos = first_row + jnp.arange(row_count, dtype=jnp.int32)
    key_pos = jnp.arange(new_keys.shape[0], dtype=jnp.int32)
    allowed_new = (key_pos[None, :] <= query_pos[:, None]) & (key_pos[None, :] < valid)
    running = attend(
        running,
        query_heads,
        head_major(new_keys, head_count),
        head_major(new_values, head_count),
        allowed_new[None],
    )
    leaf_heads = head_major(leaf_kv, head_count)
    running = attend(running, query_heads, leaf_heads[0], leaf_heads[1], True)
    running = attend_blocks(running, query_heads, branch_mine[0], branch_mine[1])
    running = attend_blocks(running, query_heads, root_full[0], root_full[1])
    largest, totals, accumulated = running
    attention = (
        jnp.transpose(accumulated / totals[:, :, None], (1, 0, 2))
        .reshape(row_count, head_count * HD)
        .astype(jnp.bfloat16)
    )
    projected = jnp.dot(attention, out_weight, preferred_element_type=jnp.float32)
    share_width = residual.shape[1]
    column = lax.axis_index("tensor") * share_width
    mid_share = (
        tensor_scatter_rows(projected, parts) + residual.astype(jnp.float32)
    ).astype(jnp.bfloat16)
    mid_full = tensor_gather_rows(mid_share, parts)
    wide_mid = mid_full.astype(jnp.float32)
    row_mean = jnp.mean(wide_mid, axis=1, keepdims=True)
    row_var = jnp.mean(wide_mid * wide_mid, axis=1, keepdims=True) - row_mean * row_mean
    normed = (
        (wide_mid - row_mean) * lax.rsqrt(row_var + NORM_EPSILON) * norm_gain + norm_bias
    ).astype(jnp.bfloat16)
    up_sum = jnp.dot(normed, up_weight, preferred_element_type=jnp.float32)
    hidden = lax.optimization_barrier(
        jax.nn.gelu(up_sum + up_bias, approximate=False).astype(jnp.bfloat16)
    )
    partial_value = jnp.dot(hidden, down_weight, preferred_element_type=jnp.float32)
    summed = tensor_scatter_rows(partial_value, parts)
    down_share = lax.dynamic_slice_in_dim(down_bias, column, share_width, 0)
    return (summed + down_share + mid_share.astype(jnp.float32)).astype(jnp.bfloat16)


def solution(mesh):
    return jax.shard_map(
        per_device,
        mesh=mesh,
        in_specs=(
            P("seq", "tensor"),
            P("seq", "tensor"),
            P("seq", "tensor"),
            P("seq", "tensor"),
            P(None, "seq", "tensor"),
            P(None, "seq", "tensor"),
            P(None, "seq", "tensor"),
            P("tensor", None),
            P(),
            P(),
            P(None, "tensor"),
            P("tensor"),
            P("tensor", None),
            P(),
            P(),
            P(),
        ),
        out_specs=P("seq", "tensor"),
        check_vma=False,
    )
```

```python
import jax
import jax.numpy as jnp
from jax import lax
from jax.sharding import PartitionSpec as P

HD = 128


NEGATIVE_FILL = -1e30
NORM_EPSILON = 1e-05
BLOCK_KEYS = 2048


def attend(running, query_heads, key_heads, value_heads, allowed):
    largest, totals, accumulated = running
    head_width = query_heads.shape[2]
    scores = jnp.einsum(
        "hqd,hkd->hqk", query_heads, key_heads, preferred_element_type=jnp.float32
    ) * head_width ** (-0.5)
    scores = jnp.where(allowed, scores, NEGATIVE_FILL)
    new_largest = jnp.maximum(largest, jnp.max(scores, axis=2))
    weights = jnp.where(allowed, jnp.exp(scores - new_largest[:, :, None]), 0.0)
    factor = jnp.exp(largest - new_largest)
    accumulated = accumulated * factor[:, :, None] + jnp.einsum(
        "hqk,hkd->hqd",
        weights.astype(jnp.bfloat16),
        value_heads,
        preferred_element_type=jnp.float32,
    )
    totals = totals * factor + jnp.sum(weights, axis=2)
    return (new_largest, totals, accumulated)


def attend_blocks(running, query_heads, key_heads, value_heads):
    for block_start in range(0, key_heads.shape[1], BLOCK_KEYS):
        running = attend(
            running,
            query_heads,
            key_heads[:, block_start : block_start + BLOCK_KEYS],
            value_heads[:, block_start : block_start + BLOCK_KEYS],
            True,
        )
    return running


def head_major(rows, head_count):
    lead = rows.shape[:-2]
    split = rows.reshape(lead + (rows.shape[-2], head_count, HD))
    order = tuple(range(len(lead))) + (len(lead) + 1, len(lead), len(lead) + 2)
    return jnp.transpose(split, order)


def tensor_sum_scatter(partial, parts):
    rows, width = partial.shape
    pieces = jnp.transpose(
        partial.astype(jnp.bfloat16).reshape(rows, parts, width // parts), (1, 0, 2)
    )
    arrived = lax.all_to_all(pieces, "tensor", 0, 0, tiled=True)
    return jnp.sum(arrived.astype(jnp.float32), axis=0)


def tensor_gather(share, parts):
    rows, width = share.shape
    copies = jnp.broadcast_to(share[None], (parts, rows, width))
    arrived = lax.all_to_all(copies, "tensor", 0, 0, tiled=True)
    return jnp.transpose(arrived, (1, 0, 2)).reshape(rows, parts * width)


def shift_pairs(shape, axis, step):
    pairs = []
    for index in range(shape[0] * shape[1] * shape[2]):
        place = [index // (shape[1] * shape[2]), (index // shape[2]) % shape[1], index % shape[2]]
        place[axis] = (place[axis] + step) % shape[axis]
        pairs.append((index, (place[0] * shape[1] + place[1]) * shape[2] + place[2]))
    return pairs


def ring_along(block, shape, axis):
    size = shape[axis]
    up = shift_pairs(shape, axis, 1)
    down = shift_pairs(shape, axis, -1)
    pieces = [block]
    from_below = block
    from_above = block
    for _ in range((size - 1) // 2):
        from_below = lax.ppermute(from_below, "seq", up)
        from_above = lax.ppermute(from_above, "seq", down)
        pieces += [from_below, from_above]
    if size % 2 == 0:
        half = block.shape[2] // 2
        first = lax.ppermute(from_below[:, :, :half], "seq", up)
        second = lax.ppermute(from_above[:, :, half:], "seq", down)
        pieces += [first, second]
    return jnp.concatenate(pieces, axis=2)


def ring_gather_seq(block, seq_size, companion):
    cores = 2
    lanes = 4
    shape = (seq_size // (lanes * cores), lanes, cores)
    gathered = ring_along(block, shape, 0)
    gathered = ring_along(gathered, shape, 1)
    gathered, companion = lax.optimization_barrier((gathered, companion))
    partner = lax.ppermute(gathered, "seq", shift_pairs(shape, 2, 1))
    return jnp.concatenate([gathered, partner], axis=2), companion


def per_device(
    residual,
    query,
    new_keys,
    new_values,
    leaf_kv,
    branch_kv,
    root_kv,
    out_weight,
    norm_gain,
    norm_bias,
    up_weight,
    up_bias,
    down_weight,
    down_bias,
    segment,
    new_len,
):
    row_count = query.shape[0]
    head_count = query.shape[1] // HD
    query_heads = head_major(query, head_count)
    device = lax.axis_index("seq")
    seq_size = lax.axis_size("seq")
    parts = lax.axis_size("tensor")
    branch_count = seq_size // 4
    feature_width = branch_kv.shape[2]

    local_rows = branch_kv.shape[1] // branch_count
    branch_local = branch_kv.reshape(2, local_rows, branch_count, feature_width)
    picked = jnp.take(branch_local, segment, axis=2)
    picked = head_major(jnp.transpose(picked, (2, 0, 1, 3)), head_count)
    arrived = lax.all_to_all(picked, "seq", 0, 0, tiled=True)

    root_full, arrived = ring_gather_seq(head_major(root_kv, head_count), seq_size, arrived)
    branch_mine = jnp.transpose(arrived, (1, 2, 0, 3, 4)).reshape(
        2, head_count, seq_size * local_rows, HD
    )

    running = (
        jnp.full((head_count, row_count), NEGATIVE_FILL, jnp.float32),
        jnp.zeros((head_count, row_count), jnp.float32),
        jnp.zeros((head_count, row_count, HD), jnp.float32),
    )
    query_pos = jnp.arange(row_count, dtype=jnp.int32)
    allowed_new = (query_pos[None, :] <= query_pos[:, None]) & (
        query_pos[None, :] < new_len[device]
    )
    running = attend(
        running,
        query_heads,
        head_major(new_keys, head_count),
        head_major(new_values, head_count),
        allowed_new[None],
    )
    leaf_heads = head_major(leaf_kv, head_count)
    running = attend(running, query_heads, leaf_heads[0], leaf_heads[1], True)
    running = attend_blocks(running, query_heads, branch_mine[0], branch_mine[1])
    running = attend_blocks(running, query_heads, root_full[0], root_full[1])
    largest, totals, accumulated = running
    attention = (
        jnp.transpose(accumulated / totals[:, :, None], (1, 0, 2))
        .reshape(row_count, head_count * HD)
        .astype(jnp.bfloat16)
    )
    projected = jnp.dot(attention, out_weight, preferred_element_type=jnp.float32)
    share_width = residual.shape[1]
    column = lax.axis_index("tensor") * share_width
    mid_share = (
        tensor_sum_scatter(projected, parts) + residual.astype(jnp.float32)
    ).astype(jnp.bfloat16)
    mid_full = tensor_gather(mid_share, parts)
    wide_mid = mid_full.astype(jnp.float32)
    row_mean = jnp.mean(wide_mid, axis=1, keepdims=True)
    row_var = jnp.mean(wide_mid * wide_mid, axis=1, keepdims=True) - row_mean * row_mean
    normed = (
        (wide_mid - row_mean) * lax.rsqrt(row_var + NORM_EPSILON) * norm_gain + norm_bias
    ).astype(jnp.bfloat16)
    up_sum = jnp.dot(normed, up_weight, preferred_element_type=jnp.float32)
    hidden = lax.optimization_barrier(
        jax.nn.gelu(up_sum + up_bias, approximate=False).astype(jnp.bfloat16)
    )
    partial_value = jnp.dot(hidden, down_weight, preferred_element_type=jnp.float32)
    summed = tensor_sum_scatter(partial_value, parts)
    down_share = lax.dynamic_slice_in_dim(down_bias, column, share_width, 0)
    return (summed + down_share + mid_share.astype(jnp.float32)).astype(jnp.bfloat16)


def solution(mesh):
    return jax.shard_map(
        per_device,
        mesh=mesh,
        in_specs=(
            P("seq", "tensor"),
            P("seq", "tensor"),
            P("seq", "tensor"),
            P("seq", "tensor"),
            P(None, "seq", "tensor"),
            P(None, "seq", "tensor"),
            P(None, "seq", "tensor"),
            P("tensor", None),
            P(),
            P(),
            P(None, "tensor"),
            P("tensor"),
            P("tensor", None),
            P(),
            P(),
            P(),
        ),
        out_specs=P("seq", "tensor"),
        check_vma=False,
    )
```

```python
import jax
import jax.numpy as jnp
from jax import lax
from jax.sharding import PartitionSpec as P

HD = 128


NEGATIVE_FILL = -1e30
NORM_EPSILON = 1e-05
BLOCK_KEYS = 2048


def attend(running, query_heads, key_heads, value_heads, allowed):
    largest, totals, accumulated = running
    head_width = query_heads.shape[2]
    scores = jnp.einsum(
        "hqd,hkd->hqk", query_heads, key_heads, preferred_element_type=jnp.float32
    ) * head_width ** (-0.5)
    scores = jnp.where(allowed, scores, NEGATIVE_FILL)
    new_largest = jnp.maximum(largest, jnp.max(scores, axis=2))
    weights = jnp.where(allowed, jnp.exp(scores - new_largest[:, :, None]), 0.0)
    factor = jnp.exp(largest - new_largest)
    accumulated = accumulated * factor[:, :, None] + jnp.einsum(
        "hqk,hkd->hqd",
        weights.astype(jnp.bfloat16),
        value_heads,
        preferred_element_type=jnp.float32,
    )
    totals = totals * factor + jnp.sum(weights, axis=2)
    return (new_largest, totals, accumulated)


def attend_blocks(running, query_heads, key_heads, value_heads):
    for block_start in range(0, key_heads.shape[1], BLOCK_KEYS):
        running = attend(
            running,
            query_heads,
            key_heads[:, block_start : block_start + BLOCK_KEYS],
            value_heads[:, block_start : block_start + BLOCK_KEYS],
            True,
        )
    return running


def head_major(rows, head_count):
    lead = rows.shape[:-2]
    split = rows.reshape(lead + (rows.shape[-2], head_count, HD))
    order = tuple(range(len(lead))) + (len(lead) + 1, len(lead), len(lead) + 2)
    return jnp.transpose(split, order)


def tensor_sum_scatter(partial, parts):
    rows, width = partial.shape
    pieces = jnp.transpose(
        partial.astype(jnp.bfloat16).reshape(rows, parts, width // parts), (1, 0, 2)
    )
    arrived = lax.all_to_all(pieces, "tensor", 0, 0, tiled=True)
    return jnp.sum(arrived.astype(jnp.float32), axis=0)


def tensor_gather(share, parts):
    rows, width = share.shape
    copies = jnp.broadcast_to(share[None], (parts, rows, width))
    arrived = lax.all_to_all(copies, "tensor", 0, 0, tiled=True)
    return jnp.transpose(arrived, (1, 0, 2)).reshape(rows, parts * width)


def shift_pairs(shape, axis, step):
    pairs = []
    for index in range(shape[0] * shape[1] * shape[2]):
        place = [index // (shape[1] * shape[2]), (index // shape[2]) % shape[1], index % shape[2]]
        place[axis] = (place[axis] + step) % shape[axis]
        pairs.append((index, (place[0] * shape[1] + place[1]) * shape[2] + place[2]))
    return pairs


def ring_along(block, shape, axis):
    size = shape[axis]
    up = shift_pairs(shape, axis, 1)
    down = shift_pairs(shape, axis, -1)
    pieces = [block]
    from_below = block
    from_above = block
    for _ in range((size - 1) // 2):
        from_below = lax.ppermute(from_below, "seq", up)
        from_above = lax.ppermute(from_above, "seq", down)
        pieces += [from_below, from_above]
    if size % 2 == 0:
        half = block.shape[2] // 2
        first = lax.ppermute(from_below[:, :, :half], "seq", up)
        second = lax.ppermute(from_above[:, :, half:], "seq", down)
        pieces += [first, second]
    return jnp.concatenate(pieces, axis=2)


def ring_gather_seq(block, seq_size, companion):
    cores = 2
    lanes = 4
    shape = (seq_size // (lanes * cores), lanes, cores)
    gathered = ring_along(block, shape, 0)
    gathered = ring_along(gathered, shape, 1)
    gathered, companion = lax.optimization_barrier((gathered, companion))
    partner = lax.ppermute(gathered, "seq", shift_pairs(shape, 2, 1))
    return jnp.concatenate([gathered, partner], axis=2), companion


def per_device(
    residual,
    query,
    new_keys,
    new_values,
    leaf_kv,
    branch_kv,
    root_kv,
    out_weight,
    norm_gain,
    norm_bias,
    up_weight,
    up_bias,
    down_weight,
    down_bias,
    segment,
    new_len,
):
    row_count = query.shape[0]
    head_count = query.shape[1] // HD
    query_heads = head_major(query, head_count)
    device = lax.axis_index("seq")
    seq_size = lax.axis_size("seq")
    parts = lax.axis_size("tensor")
    branch_count = seq_size // 4
    feature_width = branch_kv.shape[2]

    local_rows = branch_kv.shape[1] // branch_count
    branch_local = branch_kv.reshape(2, local_rows, branch_count, feature_width)
    picked = jnp.take(branch_local, segment, axis=2)
    picked = head_major(jnp.transpose(picked, (2, 0, 1, 3)), head_count)
    arrived = lax.all_to_all(picked, "seq", 0, 0, tiled=True)

    running = (
        jnp.full((head_count, row_count), NEGATIVE_FILL, jnp.float32),
        jnp.zeros((head_count, row_count), jnp.float32),
        jnp.zeros((head_count, row_count, HD), jnp.float32),
    )
    query_pos = jnp.arange(row_count, dtype=jnp.int32)
    allowed_new = (query_pos[None, :] <= query_pos[:, None]) & (
        query_pos[None, :] < new_len[device]
    )
    running = attend(
        running,
        query_heads,
        head_major(new_keys, head_count),
        head_major(new_values, head_count),
        allowed_new[None],
    )
    leaf_heads = head_major(leaf_kv, head_count)
    running = attend(running, query_heads, leaf_heads[0], leaf_heads[1], True)
    root_full, (arrived, running) = ring_gather_seq(
        head_major(root_kv, head_count), seq_size, (arrived, running)
    )
    branch_mine = jnp.transpose(arrived, (1, 2, 0, 3, 4)).reshape(
        2, head_count, seq_size * local_rows, HD
    )

    running = attend_blocks(running, query_heads, branch_mine[0], branch_mine[1])
    running = attend_blocks(running, query_heads, root_full[0], root_full[1])
    largest, totals, accumulated = running
    attention = (
        jnp.transpose(accumulated / totals[:, :, None], (1, 0, 2))
        .reshape(row_count, head_count * HD)
        .astype(jnp.bfloat16)
    )
    projected = jnp.dot(attention, out_weight, preferred_element_type=jnp.float32)
    share_width = residual.shape[1]
    column = lax.axis_index("tensor") * share_width
    mid_share = (
        tensor_sum_scatter(projected, parts) + residual.astype(jnp.float32)
    ).astype(jnp.bfloat16)
    mid_full = tensor_gather(mid_share, parts)
    wide_mid = mid_full.astype(jnp.float32)
    row_mean = jnp.mean(wide_mid, axis=1, keepdims=True)
    row_var = jnp.mean(wide_mid * wide_mid, axis=1, keepdims=True) - row_mean * row_mean
    normed = (
        (wide_mid - row_mean) * lax.rsqrt(row_var + NORM_EPSILON) * norm_gain + norm_bias
    ).astype(jnp.bfloat16)
    up_sum = jnp.dot(normed, up_weight, preferred_element_type=jnp.float32)
    hidden = lax.optimization_barrier(
        jax.nn.gelu(up_sum + up_bias, approximate=False).astype(jnp.bfloat16)
    )
    partial_value = jnp.dot(hidden, down_weight, preferred_element_type=jnp.float32)
    summed = tensor_sum_scatter(partial_value, parts)
    down_share = lax.dynamic_slice_in_dim(down_bias, column, share_width, 0)
    return (summed + down_share + mid_share.astype(jnp.float32)).astype(jnp.bfloat16)


def solution(mesh):
    return jax.shard_map(
        per_device,
        mesh=mesh,
        in_specs=(
            P("seq", "tensor"),
            P("seq", "tensor"),
            P("seq", "tensor"),
            P("seq", "tensor"),
            P(None, "seq", "tensor"),
            P(None, "seq", "tensor"),
            P(None, "seq", "tensor"),
            P("tensor", None),
            P(),
            P(),
            P(None, "tensor"),
            P("tensor"),
            P("tensor", None),
            P(),
            P(),
            P(),
        ),
        out_specs=P("seq", "tensor"),
        check_vma=False,
    )
```

```python
import jax
import jax.numpy as jnp
from jax import lax
from jax.sharding import PartitionSpec as P

HD = 128


NEGATIVE_FILL = -1e30
NORM_EPSILON = 1e-05
BLOCK_KEYS = 2048


def attend(running, query_heads, key_heads, value_heads, allowed):
    largest, totals, accumulated = running
    head_width = query_heads.shape[2]
    scores = jnp.einsum(
        "hqd,hkd->hqk", query_heads, key_heads, preferred_element_type=jnp.float32
    ) * head_width ** (-0.5)
    scores = jnp.where(allowed, scores, NEGATIVE_FILL)
    new_largest = jnp.maximum(largest, jnp.max(scores, axis=2))
    weights = jnp.where(allowed, jnp.exp(scores - new_largest[:, :, None]), 0.0)
    factor = jnp.exp(largest - new_largest)
    accumulated = accumulated * factor[:, :, None] + jnp.einsum(
        "hqk,hkd->hqd",
        weights.astype(jnp.bfloat16),
        value_heads,
        preferred_element_type=jnp.float32,
    )
    totals = totals * factor + jnp.sum(weights, axis=2)
    return (new_largest, totals, accumulated)


def attend_blocks(running, query_heads, key_heads, value_heads):
    for block_start in range(0, key_heads.shape[1], BLOCK_KEYS):
        running = attend(
            running,
            query_heads,
            key_heads[:, block_start : block_start + BLOCK_KEYS],
            value_heads[:, block_start : block_start + BLOCK_KEYS],
            True,
        )
    return running


def head_major(rows, head_count):
    lead = rows.shape[:-2]
    split = rows.reshape(lead + (rows.shape[-2], head_count, HD))
    order = tuple(range(len(lead))) + (len(lead) + 1, len(lead), len(lead) + 2)
    return jnp.transpose(split, order)


def tensor_sum_scatter(partial, parts):
    rows, width = partial.shape
    pieces = jnp.transpose(
        partial.astype(jnp.bfloat16).reshape(rows, parts, width // parts), (1, 0, 2)
    )
    arrived = lax.all_to_all(pieces, "tensor", 0, 0, tiled=True)
    return jnp.sum(arrived.astype(jnp.float32), axis=0)


def tensor_gather(share, parts):
    rows, width = share.shape
    copies = jnp.broadcast_to(share[None], (parts, rows, width))
    arrived = lax.all_to_all(copies, "tensor", 0, 0, tiled=True)
    return jnp.transpose(arrived, (1, 0, 2)).reshape(rows, parts * width)


def shift_pairs(shape, axis, step):
    pairs = []
    for index in range(shape[0] * shape[1] * shape[2]):
        place = [index // (shape[1] * shape[2]), (index // shape[2]) % shape[1], index % shape[2]]
        place[axis] = (place[axis] + step) % shape[axis]
        pairs.append((index, (place[0] * shape[1] + place[1]) * shape[2] + place[2]))
    return pairs


def ring_along(block, shape, axis):
    size = shape[axis]
    up = shift_pairs(shape, axis, 1)
    down = shift_pairs(shape, axis, -1)
    pieces = [block]
    from_below = block
    from_above = block
    for _ in range((size - 1) // 2):
        from_below = lax.ppermute(from_below, "seq", up)
        from_above = lax.ppermute(from_above, "seq", down)
        pieces += [from_below, from_above]
    if size % 2 == 0:
        half = block.shape[2] // 2
        first = lax.ppermute(from_below[:, :, :half], "seq", up)
        second = lax.ppermute(from_above[:, :, half:], "seq", down)
        pieces += [first, second]
    return jnp.concatenate(pieces, axis=2)


def ring_gather_seq(block, seq_size, companion):
    cores = 2
    lanes = 4
    shape = (seq_size // (lanes * cores), lanes, cores)
    gathered = ring_along(block, shape, 0)
    gathered = ring_along(gathered, shape, 1)
    gathered, companion = lax.optimization_barrier((gathered, companion))
    partner = lax.ppermute(gathered, "seq", shift_pairs(shape, 2, 1))
    return (gathered, partner), companion


def per_device(
    residual,
    query,
    new_keys,
    new_values,
    leaf_kv,
    branch_kv,
    root_kv,
    out_weight,
    norm_gain,
    norm_bias,
    up_weight,
    up_bias,
    down_weight,
    down_bias,
    segment,
    new_len,
):
    row_count = query.shape[0]
    head_count = query.shape[1] // HD
    query_heads = head_major(query, head_count)
    device = lax.axis_index("seq")
    seq_size = lax.axis_size("seq")
    parts = lax.axis_size("tensor")
    branch_count = seq_size // 4
    feature_width = branch_kv.shape[2]

    local_rows = branch_kv.shape[1] // branch_count
    branch_local = branch_kv.reshape(2, local_rows, branch_count, feature_width)
    picked = jnp.take(branch_local, segment, axis=2)
    picked = head_major(jnp.transpose(picked, (2, 0, 1, 3)), head_count)
    arrived = lax.all_to_all(picked, "seq", 0, 0, tiled=True)

    running = (
        jnp.full((head_count, row_count), NEGATIVE_FILL, jnp.float32),
        jnp.zeros((head_count, row_count), jnp.float32),
        jnp.zeros((head_count, row_count, HD), jnp.float32),
    )
    query_pos = jnp.arange(row_count, dtype=jnp.int32)
    allowed_new = (query_pos[None, :] <= query_pos[:, None]) & (
        query_pos[None, :] < new_len[device]
    )
    running = attend(
        running,
        query_heads,
        head_major(new_keys, head_count),
        head_major(new_values, head_count),
        allowed_new[None],
    )
    leaf_heads = head_major(leaf_kv, head_count)
    running = attend(running, query_heads, leaf_heads[0], leaf_heads[1], True)
    root_full, (arrived, running) = ring_gather_seq(
        head_major(root_kv, head_count), seq_size, (arrived, running)
    )
    branch_mine = jnp.transpose(arrived, (1, 2, 0, 3, 4)).reshape(
        2, head_count, seq_size * local_rows, HD
    )

    root_own, root_partner = root_full
    running = attend_blocks(running, query_heads, root_own[0], root_own[1])
    running = attend_blocks(running, query_heads, branch_mine[0], branch_mine[1])
    running = attend_blocks(running, query_heads, root_partner[0], root_partner[1])
    largest, totals, accumulated = running
    attention = (
        jnp.transpose(accumulated / totals[:, :, None], (1, 0, 2))
        .reshape(row_count, head_count * HD)
        .astype(jnp.bfloat16)
    )
    projected = jnp.dot(attention, out_weight, preferred_element_type=jnp.float32)
    share_width = residual.shape[1]
    column = lax.axis_index("tensor") * share_width
    mid_share = (
        tensor_sum_scatter(projected, parts) + residual.astype(jnp.float32)
    ).astype(jnp.bfloat16)
    mid_full = tensor_gather(mid_share, parts)
    wide_mid = mid_full.astype(jnp.float32)
    row_mean = jnp.mean(wide_mid, axis=1, keepdims=True)
    row_var = jnp.mean(wide_mid * wide_mid, axis=1, keepdims=True) - row_mean * row_mean
    normed = (
        (wide_mid - row_mean) * lax.rsqrt(row_var + NORM_EPSILON) * norm_gain + norm_bias
    ).astype(jnp.bfloat16)
    up_sum = jnp.dot(normed, up_weight, preferred_element_type=jnp.float32)
    hidden = lax.optimization_barrier(
        jax.nn.gelu(up_sum + up_bias, approximate=False).astype(jnp.bfloat16)
    )
    partial_value = jnp.dot(hidden, down_weight, preferred_element_type=jnp.float32)
    summed = tensor_sum_scatter(partial_value, parts)
    down_share = lax.dynamic_slice_in_dim(down_bias, column, share_width, 0)
    return (summed + down_share + mid_share.astype(jnp.float32)).astype(jnp.bfloat16)


def solution(mesh):
    return jax.shard_map(
        per_device,
        mesh=mesh,
        in_specs=(
            P("seq", "tensor"),
            P("seq", "tensor"),
            P("seq", "tensor"),
            P("seq", "tensor"),
            P(None, "seq", "tensor"),
            P(None, "seq", "tensor"),
            P(None, "seq", "tensor"),
            P("tensor", None),
            P(),
            P(),
            P(None, "tensor"),
            P("tensor"),
            P("tensor", None),
            P(),
            P(),
            P(),
        ),
        out_specs=P("seq", "tensor"),
        check_vma=False,
    )
```

```python
import jax
import jax.numpy as jnp
from jax import lax
from jax.sharding import PartitionSpec as P

HD = 128


NEGATIVE_FILL = -1e30
NORM_EPSILON = 1e-05
BLOCK_KEYS = 1024


def attend(running, query_heads, key_heads, value_heads, allowed):
    largest, totals, accumulated = running
    head_width = query_heads.shape[2]
    scores = jnp.einsum(
        "hqd,hkd->hqk", query_heads, key_heads, preferred_element_type=jnp.float32
    ) * head_width ** (-0.5)
    scores = jnp.where(allowed, scores, NEGATIVE_FILL)
    new_largest = jnp.maximum(largest, jnp.max(scores, axis=2))
    weights = jnp.where(allowed, jnp.exp(scores - new_largest[:, :, None]), 0.0)
    factor = jnp.exp(largest - new_largest)
    accumulated = accumulated * factor[:, :, None] + jnp.einsum(
        "hqk,hkd->hqd",
        weights.astype(jnp.bfloat16),
        value_heads,
        preferred_element_type=jnp.float32,
    )
    totals = totals * factor + jnp.sum(weights, axis=2)
    return (new_largest, totals, accumulated)


def attend_blocks(running, query_heads, key_heads, value_heads):
    for block_start in range(0, key_heads.shape[1], BLOCK_KEYS):
        running = attend(
            running,
            query_heads,
            key_heads[:, block_start : block_start + BLOCK_KEYS],
            value_heads[:, block_start : block_start + BLOCK_KEYS],
            True,
        )
    return running


def head_major(rows, head_count):
    lead = rows.shape[:-2]
    split = rows.reshape(lead + (rows.shape[-2], head_count, HD))
    order = tuple(range(len(lead))) + (len(lead) + 1, len(lead), len(lead) + 2)
    return jnp.transpose(split, order)


def tensor_sum_scatter(partial, parts):
    rows, width = partial.shape
    pieces = jnp.transpose(
        partial.astype(jnp.bfloat16).reshape(rows, parts, width // parts), (1, 0, 2)
    )
    arrived = lax.all_to_all(pieces, "tensor", 0, 0, tiled=True)
    return jnp.sum(arrived.astype(jnp.float32), axis=0)


def tensor_gather(share, parts):
    rows, width = share.shape
    copies = jnp.broadcast_to(share[None], (parts, rows, width))
    arrived = lax.all_to_all(copies, "tensor", 0, 0, tiled=True)
    return jnp.transpose(arrived, (1, 0, 2)).reshape(rows, parts * width)


def shift_pairs(shape, axis, step):
    pairs = []
    for index in range(shape[0] * shape[1] * shape[2]):
        place = [index // (shape[1] * shape[2]), (index // shape[2]) % shape[1], index % shape[2]]
        place[axis] = (place[axis] + step) % shape[axis]
        pairs.append((index, (place[0] * shape[1] + place[1]) * shape[2] + place[2]))
    return pairs


def ring_along(block, shape, axis):
    size = shape[axis]
    up = shift_pairs(shape, axis, 1)
    down = shift_pairs(shape, axis, -1)
    pieces = [block]
    from_below = block
    from_above = block
    for _ in range((size - 1) // 2):
        from_below = lax.ppermute(from_below, "seq", up)
        from_above = lax.ppermute(from_above, "seq", down)
        pieces += [from_below, from_above]
    if size % 2 == 0:
        half = block.shape[2] // 2
        first = lax.ppermute(from_below[:, :, :half], "seq", up)
        second = lax.ppermute(from_above[:, :, half:], "seq", down)
        pieces += [first, second]
    return jnp.concatenate(pieces, axis=2)


def ring_gather_seq(block, seq_size, companion):
    cores = 2
    lanes = 4
    shape = (seq_size // (lanes * cores), lanes, cores)
    gathered = ring_along(block, shape, 0)
    gathered = ring_along(gathered, shape, 1)
    gathered, companion = lax.optimization_barrier((gathered, companion))
    partner = lax.ppermute(gathered, "seq", shift_pairs(shape, 2, 1))
    return jnp.concatenate([gathered, partner], axis=2), companion


def per_device(
    residual,
    query,
    new_keys,
    new_values,
    leaf_kv,
    branch_kv,
    root_kv,
    out_weight,
    norm_gain,
    norm_bias,
    up_weight,
    up_bias,
    down_weight,
    down_bias,
    segment,
    new_len,
):
    row_count = query.shape[0]
    head_count = query.shape[1] // HD
    query_heads = head_major(query, head_count)
    device = lax.axis_index("seq")
    seq_size = lax.axis_size("seq")
    parts = lax.axis_size("tensor")
    branch_count = seq_size // 4
    feature_width = branch_kv.shape[2]

    local_rows = branch_kv.shape[1] // branch_count
    branch_local = branch_kv.reshape(2, local_rows, branch_count, feature_width)
    picked = jnp.take(branch_local, segment, axis=2)
    picked = head_major(jnp.transpose(picked, (2, 0, 1, 3)), head_count)
    arrived = lax.all_to_all(picked, "seq", 0, 0, tiled=True)

    running = (
        jnp.full((head_count, row_count), NEGATIVE_FILL, jnp.float32),
        jnp.zeros((head_count, row_count), jnp.float32),
        jnp.zeros((head_count, row_count, HD), jnp.float32),
    )
    query_pos = jnp.arange(row_count, dtype=jnp.int32)
    allowed_new = (query_pos[None, :] <= query_pos[:, None]) & (
        query_pos[None, :] < new_len[device]
    )
    running = attend(
        running,
        query_heads,
        head_major(new_keys, head_count),
        head_major(new_values, head_count),
        allowed_new[None],
    )
    leaf_heads = head_major(leaf_kv, head_count)
    running = attend(running, query_heads, leaf_heads[0], leaf_heads[1], True)
    root_full, (arrived, running) = ring_gather_seq(
        head_major(root_kv, head_count), seq_size, (arrived, running)
    )
    branch_mine = jnp.transpose(arrived, (1, 2, 0, 3, 4)).reshape(
        2, head_count, seq_size * local_rows, HD
    )

    running = attend_blocks(running, query_heads, branch_mine[0], branch_mine[1])
    running = attend_blocks(running, query_heads, root_full[0], root_full[1])
    largest, totals, accumulated = running
    attention = (
        jnp.transpose(accumulated / totals[:, :, None], (1, 0, 2))
        .reshape(row_count, head_count * HD)
        .astype(jnp.bfloat16)
    )
    projected = jnp.dot(attention, out_weight, preferred_element_type=jnp.float32)
    share_width = residual.shape[1]
    column = lax.axis_index("tensor") * share_width
    mid_share = (
        tensor_sum_scatter(projected, parts) + residual.astype(jnp.float32)
    ).astype(jnp.bfloat16)
    mid_full = tensor_gather(mid_share, parts)
    wide_mid = mid_full.astype(jnp.float32)
    row_mean = jnp.mean(wide_mid, axis=1, keepdims=True)
    row_var = jnp.mean(wide_mid * wide_mid, axis=1, keepdims=True) - row_mean * row_mean
    normed = (
        (wide_mid - row_mean) * lax.rsqrt(row_var + NORM_EPSILON) * norm_gain + norm_bias
    ).astype(jnp.bfloat16)
    up_sum = jnp.dot(normed, up_weight, preferred_element_type=jnp.float32)
    hidden = lax.optimization_barrier(
        jax.nn.gelu(up_sum + up_bias, approximate=False).astype(jnp.bfloat16)
    )
    partial_value = jnp.dot(hidden, down_weight, preferred_element_type=jnp.float32)
    summed = tensor_sum_scatter(partial_value, parts)
    down_share = lax.dynamic_slice_in_dim(down_bias, column, share_width, 0)
    return (summed + down_share + mid_share.astype(jnp.float32)).astype(jnp.bfloat16)


def solution(mesh):
    return jax.shard_map(
        per_device,
        mesh=mesh,
        in_specs=(
            P("seq", "tensor"),
            P("seq", "tensor"),
            P("seq", "tensor"),
            P("seq", "tensor"),
            P(None, "seq", "tensor"),
            P(None, "seq", "tensor"),
            P(None, "seq", "tensor"),
            P("tensor", None),
            P(),
            P(),
            P(None, "tensor"),
            P("tensor"),
            P("tensor", None),
            P(),
            P(),
            P(),
        ),
        out_specs=P("seq", "tensor"),
        check_vma=False,
    )
```

```python
import jax
import jax.numpy as jnp
from jax import lax
from jax.sharding import PartitionSpec as P

HD = 128


NEGATIVE_FILL = -1e30
NORM_EPSILON = 1e-05
BLOCK_KEYS = 2048


def attend(running, query_heads, key_heads, value_heads, allowed):
    largest, totals, accumulated = running
    head_width = query_heads.shape[2]
    scores = jnp.einsum(
        "hqd,hkd->hqk", query_heads, key_heads, preferred_element_type=jnp.float32
    ) * head_width ** (-0.5)
    scores = jnp.where(allowed, scores, NEGATIVE_FILL)
    new_largest = jnp.maximum(largest, jnp.max(scores, axis=2))
    weights = jnp.where(allowed, jnp.exp(scores - new_largest[:, :, None]), 0.0)
    factor = jnp.exp(largest - new_largest)
    accumulated = accumulated * factor[:, :, None] + jnp.einsum(
        "hqk,hkd->hqd",
        weights.astype(jnp.bfloat16),
        value_heads,
        preferred_element_type=jnp.float32,
    )
    totals = totals * factor + jnp.sum(weights, axis=2)
    return (new_largest, totals, accumulated)


def attend_blocks(running, query_heads, key_heads, value_heads):
    for block_start in range(0, key_heads.shape[1], BLOCK_KEYS):
        running = attend(
            running,
            query_heads,
            key_heads[:, block_start : block_start + BLOCK_KEYS],
            value_heads[:, block_start : block_start + BLOCK_KEYS],
            True,
        )
    return running


def head_major(rows, head_count):
    lead = rows.shape[:-2]
    split = rows.reshape(lead + (rows.shape[-2], head_count, HD))
    order = tuple(range(len(lead))) + (len(lead) + 1, len(lead), len(lead) + 2)
    return jnp.transpose(split, order)


def tensor_sum_scatter(partial, parts):
    rows, width = partial.shape
    pieces = jnp.transpose(
        partial.astype(jnp.bfloat16).reshape(rows, parts, width // parts), (1, 0, 2)
    )
    arrived = lax.all_to_all(pieces, "tensor", 0, 0, tiled=True)
    return jnp.sum(arrived.astype(jnp.float32), axis=0)


def tensor_gather(share, parts):
    rows, width = share.shape
    copies = jnp.broadcast_to(share[None], (parts, rows, width))
    arrived = lax.all_to_all(copies, "tensor", 0, 0, tiled=True)
    return jnp.transpose(arrived, (1, 0, 2)).reshape(rows, parts * width)


def shift_pairs(shape, axis, step):
    pairs = []
    for index in range(shape[0] * shape[1] * shape[2]):
        place = [index // (shape[1] * shape[2]), (index // shape[2]) % shape[1], index % shape[2]]
        place[axis] = (place[axis] + step) % shape[axis]
        pairs.append((index, (place[0] * shape[1] + place[1]) * shape[2] + place[2]))
    return pairs


def ring_along(block, shape, axis):
    size = shape[axis]
    up = shift_pairs(shape, axis, 1)
    down = shift_pairs(shape, axis, -1)
    pieces = [block]
    from_below = block
    from_above = block
    for _ in range((size - 1) // 2):
        from_below = lax.ppermute(from_below, "seq", up)
        from_above = lax.ppermute(from_above, "seq", down)
        pieces += [from_below, from_above]
    if size % 2 == 0:
        half = block.shape[2] // 2
        first = lax.ppermute(from_below[:, :, :half], "seq", up)
        second = lax.ppermute(from_above[:, :, half:], "seq", down)
        pieces += [first, second]
    return jnp.concatenate(pieces, axis=2)


def ring_gather_seq(block, seq_size, companion):
    cores = 2
    lanes = 4
    shape = (seq_size // (lanes * cores), lanes, cores)
    gathered = ring_along(block, shape, 0)
    gathered, companion = lax.optimization_barrier((gathered, companion))
    gathered = ring_along(gathered, shape, 1)
    partner = lax.ppermute(gathered, "seq", shift_pairs(shape, 2, 1))
    return jnp.concatenate([gathered, partner], axis=2), companion


def per_device(
    residual,
    query,
    new_keys,
    new_values,
    leaf_kv,
    branch_kv,
    root_kv,
    out_weight,
    norm_gain,
    norm_bias,
    up_weight,
    up_bias,
    down_weight,
    down_bias,
    segment,
    new_len,
):
    row_count = query.shape[0]
    head_count = query.shape[1] // HD
    query_heads = head_major(query, head_count)
    device = lax.axis_index("seq")
    seq_size = lax.axis_size("seq")
    parts = lax.axis_size("tensor")
    branch_count = seq_size // 4
    feature_width = branch_kv.shape[2]

    local_rows = branch_kv.shape[1] // branch_count
    branch_local = branch_kv.reshape(2, local_rows, branch_count, feature_width)
    picked = jnp.take(branch_local, segment, axis=2)
    picked = head_major(jnp.transpose(picked, (2, 0, 1, 3)), head_count)
    arrived = lax.all_to_all(picked, "seq", 0, 0, tiled=True)

    running = (
        jnp.full((head_count, row_count), NEGATIVE_FILL, jnp.float32),
        jnp.zeros((head_count, row_count), jnp.float32),
        jnp.zeros((head_count, row_count, HD), jnp.float32),
    )
    query_pos = jnp.arange(row_count, dtype=jnp.int32)
    allowed_new = (query_pos[None, :] <= query_pos[:, None]) & (
        query_pos[None, :] < new_len[device]
    )
    running = attend(
        running,
        query_heads,
        head_major(new_keys, head_count),
        head_major(new_values, head_count),
        allowed_new[None],
    )
    leaf_heads = head_major(leaf_kv, head_count)
    running = attend(running, query_heads, leaf_heads[0], leaf_heads[1], True)
    root_full, (arrived, running) = ring_gather_seq(
        head_major(root_kv, head_count), seq_size, (arrived, running)
    )
    branch_mine = jnp.transpose(arrived, (1, 2, 0, 3, 4)).reshape(
        2, head_count, seq_size * local_rows, HD
    )

    running = attend_blocks(running, query_heads, branch_mine[0], branch_mine[1])
    running = attend_blocks(running, query_heads, root_full[0], root_full[1])
    largest, totals, accumulated = running
    attention = (
        jnp.transpose(accumulated / totals[:, :, None], (1, 0, 2))
        .reshape(row_count, head_count * HD)
        .astype(jnp.bfloat16)
    )
    projected = jnp.dot(attention, out_weight, preferred_element_type=jnp.float32)
    share_width = residual.shape[1]
    column = lax.axis_index("tensor") * share_width
    mid_share = (
        tensor_sum_scatter(projected, parts) + residual.astype(jnp.float32)
    ).astype(jnp.bfloat16)
    mid_full = tensor_gather(mid_share, parts)
    wide_mid = mid_full.astype(jnp.float32)
    row_mean = jnp.mean(wide_mid, axis=1, keepdims=True)
    row_var = jnp.mean(wide_mid * wide_mid, axis=1, keepdims=True) - row_mean * row_mean
    normed = (
        (wide_mid - row_mean) * lax.rsqrt(row_var + NORM_EPSILON) * norm_gain + norm_bias
    ).astype(jnp.bfloat16)
    up_sum = jnp.dot(normed, up_weight, preferred_element_type=jnp.float32)
    hidden = lax.optimization_barrier(
        jax.nn.gelu(up_sum + up_bias, approximate=False).astype(jnp.bfloat16)
    )
    partial_value = jnp.dot(hidden, down_weight, preferred_element_type=jnp.float32)
    summed = tensor_sum_scatter(partial_value, parts)
    down_share = lax.dynamic_slice_in_dim(down_bias, column, share_width, 0)
    return (summed + down_share + mid_share.astype(jnp.float32)).astype(jnp.bfloat16)


def solution(mesh):
    return jax.shard_map(
        per_device,
        mesh=mesh,
        in_specs=(
            P("seq", "tensor"),
            P("seq", "tensor"),
            P("seq", "tensor"),
            P("seq", "tensor"),
            P(None, "seq", "tensor"),
            P(None, "seq", "tensor"),
            P(None, "seq", "tensor"),
            P("tensor", None),
            P(),
            P(),
            P(None, "tensor"),
            P("tensor"),
            P("tensor", None),
            P(),
            P(),
            P(),
        ),
        out_specs=P("seq", "tensor"),
        check_vma=False,
    )
```

```python
import jax
import jax.numpy as jnp
from jax import lax
from jax.sharding import PartitionSpec as P

HD = 128


NEGATIVE_FILL = -1e30
NORM_EPSILON = 1e-05
BLOCK_KEYS = 2048


def attend(running, query_heads, key_heads, value_heads, allowed):
    largest, totals, accumulated = running
    head_width = query_heads.shape[2]
    scores = jnp.einsum(
        "hqd,hkd->hqk", query_heads, key_heads, preferred_element_type=jnp.float32
    ) * head_width ** (-0.5)
    scores = jnp.where(allowed, scores, NEGATIVE_FILL)
    new_largest = jnp.maximum(largest, jnp.max(scores, axis=2))
    weights = jnp.where(allowed, jnp.exp(scores - new_largest[:, :, None]), 0.0)
    factor = jnp.exp(largest - new_largest)
    accumulated = accumulated * factor[:, :, None] + jnp.einsum(
        "hqk,hkd->hqd",
        weights.astype(jnp.bfloat16),
        value_heads,
        preferred_element_type=jnp.float32,
    )
    totals = totals * factor + jnp.sum(weights, axis=2)
    return (new_largest, totals, accumulated)


def attend_blocks(running, query_heads, key_heads, value_heads):
    for block_start in range(0, key_heads.shape[1], BLOCK_KEYS):
        running = attend(
            running,
            query_heads,
            key_heads[:, block_start : block_start + BLOCK_KEYS],
            value_heads[:, block_start : block_start + BLOCK_KEYS],
            True,
        )
    return running


def head_major(rows, head_count):
    lead = rows.shape[:-2]
    split = rows.reshape(lead + (rows.shape[-2], head_count, HD))
    order = tuple(range(len(lead))) + (len(lead) + 1, len(lead), len(lead) + 2)
    return jnp.transpose(split, order)


def tensor_sum_scatter(partial, parts):
    rows, width = partial.shape
    pieces = jnp.transpose(
        partial.astype(jnp.bfloat16).reshape(rows, parts, width // parts), (1, 0, 2)
    )
    arrived = lax.all_to_all(pieces, "tensor", 0, 0, tiled=True)
    return jnp.sum(arrived.astype(jnp.float32), axis=0)


def tensor_gather(share, parts):
    rows, width = share.shape
    copies = jnp.broadcast_to(share[None], (parts, rows, width))
    arrived = lax.all_to_all(copies, "tensor", 0, 0, tiled=True)
    return jnp.transpose(arrived, (1, 0, 2)).reshape(rows, parts * width)


def shift_pairs(shape, axis, step):
    pairs = []
    for index in range(shape[0] * shape[1] * shape[2]):
        place = [index // (shape[1] * shape[2]), (index // shape[2]) % shape[1], index % shape[2]]
        place[axis] = (place[axis] + step) % shape[axis]
        pairs.append((index, (place[0] * shape[1] + place[1]) * shape[2] + place[2]))
    return pairs


def ring_along(block, shape, axis):
    size = shape[axis]
    up = shift_pairs(shape, axis, 1)
    down = shift_pairs(shape, axis, -1)
    pieces = [block]
    from_below = block
    from_above = block
    for _ in range((size - 1) // 2):
        from_below = lax.ppermute(from_below, "seq", up)
        from_above = lax.ppermute(from_above, "seq", down)
        pieces += [from_below, from_above]
    if size % 2 == 0:
        half = block.shape[2] // 2
        first = lax.ppermute(from_below[:, :, :half], "seq", up)
        second = lax.ppermute(from_above[:, :, half:], "seq", down)
        pieces += [first, second]
    return jnp.concatenate(pieces, axis=2)


def ring_gather_seq(block, seq_size, companion):
    cores = 2
    lanes = 4
    shape = (seq_size // (lanes * cores), lanes, cores)
    transfer, work = companion
    gathered = ring_along(block, shape, 0)
    gathered, transfer = lax.optimization_barrier((gathered, transfer))
    gathered = ring_along(gathered, shape, 1)
    gathered, work = lax.optimization_barrier((gathered, work))
    companion = (transfer, work)
    partner = lax.ppermute(gathered, "seq", shift_pairs(shape, 2, 1))
    return jnp.concatenate([gathered, partner], axis=2), companion


def per_device(
    residual,
    query,
    new_keys,
    new_values,
    leaf_kv,
    branch_kv,
    root_kv,
    out_weight,
    norm_gain,
    norm_bias,
    up_weight,
    up_bias,
    down_weight,
    down_bias,
    segment,
    new_len,
):
    row_count = query.shape[0]
    head_count = query.shape[1] // HD
    query_heads = head_major(query, head_count)
    device = lax.axis_index("seq")
    seq_size = lax.axis_size("seq")
    parts = lax.axis_size("tensor")
    branch_count = seq_size // 4
    feature_width = branch_kv.shape[2]

    local_rows = branch_kv.shape[1] // branch_count
    branch_local = branch_kv.reshape(2, local_rows, branch_count, feature_width)
    picked = jnp.take(branch_local, segment, axis=2)
    picked = head_major(jnp.transpose(picked, (2, 0, 1, 3)), head_count)
    arrived = lax.all_to_all(picked, "seq", 0, 0, tiled=True)

    running = (
        jnp.full((head_count, row_count), NEGATIVE_FILL, jnp.float32),
        jnp.zeros((head_count, row_count), jnp.float32),
        jnp.zeros((head_count, row_count, HD), jnp.float32),
    )
    query_pos = jnp.arange(row_count, dtype=jnp.int32)
    allowed_new = (query_pos[None, :] <= query_pos[:, None]) & (
        query_pos[None, :] < new_len[device]
    )
    running = attend(
        running,
        query_heads,
        head_major(new_keys, head_count),
        head_major(new_values, head_count),
        allowed_new[None],
    )
    leaf_heads = head_major(leaf_kv, head_count)
    running = attend(running, query_heads, leaf_heads[0], leaf_heads[1], True)
    root_full, (arrived, running) = ring_gather_seq(
        head_major(root_kv, head_count), seq_size, (arrived, running)
    )
    branch_mine = jnp.transpose(arrived, (1, 2, 0, 3, 4)).reshape(
        2, head_count, seq_size * local_rows, HD
    )

    running = attend_blocks(running, query_heads, branch_mine[0], branch_mine[1])
    running = attend_blocks(running, query_heads, root_full[0], root_full[1])
    largest, totals, accumulated = running
    attention = (
        jnp.transpose(accumulated / totals[:, :, None], (1, 0, 2))
        .reshape(row_count, head_count * HD)
        .astype(jnp.bfloat16)
    )
    projected = jnp.dot(attention, out_weight, preferred_element_type=jnp.float32)
    share_width = residual.shape[1]
    column = lax.axis_index("tensor") * share_width
    mid_share = (
        tensor_sum_scatter(projected, parts) + residual.astype(jnp.float32)
    ).astype(jnp.bfloat16)
    mid_full = tensor_gather(mid_share, parts)
    wide_mid = mid_full.astype(jnp.float32)
    row_mean = jnp.mean(wide_mid, axis=1, keepdims=True)
    row_var = jnp.mean(wide_mid * wide_mid, axis=1, keepdims=True) - row_mean * row_mean
    normed = (
        (wide_mid - row_mean) * lax.rsqrt(row_var + NORM_EPSILON) * norm_gain + norm_bias
    ).astype(jnp.bfloat16)
    up_sum = jnp.dot(normed, up_weight, preferred_element_type=jnp.float32)
    hidden = lax.optimization_barrier(
        jax.nn.gelu(up_sum + up_bias, approximate=False).astype(jnp.bfloat16)
    )
    partial_value = jnp.dot(hidden, down_weight, preferred_element_type=jnp.float32)
    summed = tensor_sum_scatter(partial_value, parts)
    down_share = lax.dynamic_slice_in_dim(down_bias, column, share_width, 0)
    return (summed + down_share + mid_share.astype(jnp.float32)).astype(jnp.bfloat16)


def solution(mesh):
    return jax.shard_map(
        per_device,
        mesh=mesh,
        in_specs=(
            P("seq", "tensor"),
            P("seq", "tensor"),
            P("seq", "tensor"),
            P("seq", "tensor"),
            P(None, "seq", "tensor"),
            P(None, "seq", "tensor"),
            P(None, "seq", "tensor"),
            P("tensor", None),
            P(),
            P(),
            P(None, "tensor"),
            P("tensor"),
            P("tensor", None),
            P(),
            P(),
            P(),
        ),
        out_specs=P("seq", "tensor"),
        check_vma=False,
    )
```

```python
import jax
import jax.numpy as jnp
from jax import lax
from jax.sharding import PartitionSpec as P

HD = 128


NEGATIVE_FILL = -1e30
NORM_EPSILON = 1e-05
BLOCK_KEYS = 2048


def attend(running, query_heads, key_heads, value_heads, allowed):
    largest, totals, accumulated = running
    head_width = query_heads.shape[2]
    scores = jnp.einsum(
        "hqd,hkd->hqk", query_heads, key_heads, preferred_element_type=jnp.float32
    ) * head_width ** (-0.5)
    scores = jnp.where(allowed, scores, NEGATIVE_FILL)
    new_largest = jnp.maximum(largest, jnp.max(scores, axis=2))
    weights = jnp.where(allowed, jnp.exp(scores - new_largest[:, :, None]), 0.0)
    factor = jnp.exp(largest - new_largest)
    accumulated = accumulated * factor[:, :, None] + jnp.einsum(
        "hqk,hkd->hqd",
        weights.astype(jnp.bfloat16),
        value_heads,
        preferred_element_type=jnp.float32,
    )
    totals = totals * factor + jnp.sum(weights, axis=2)
    return (new_largest, totals, accumulated)


def attend_blocks(running, query_heads, key_heads, value_heads):
    for block_start in range(0, key_heads.shape[1], BLOCK_KEYS):
        running = attend(
            running,
            query_heads,
            key_heads[:, block_start : block_start + BLOCK_KEYS],
            value_heads[:, block_start : block_start + BLOCK_KEYS],
            True,
        )
    return running


def head_major(rows, head_count):
    lead = rows.shape[:-2]
    split = rows.reshape(lead + (rows.shape[-2], head_count, HD))
    order = tuple(range(len(lead))) + (len(lead) + 1, len(lead), len(lead) + 2)
    return jnp.transpose(split, order)


def tensor_sum_scatter(partial, parts):
    rows, width = partial.shape
    pieces = jnp.transpose(
        partial.astype(jnp.bfloat16).reshape(rows, parts, width // parts), (1, 0, 2)
    )
    arrived = lax.all_to_all(pieces, "tensor", 0, 0, tiled=True)
    return jnp.sum(arrived.astype(jnp.float32), axis=0)


def tensor_gather(share, parts):
    rows, width = share.shape
    copies = jnp.broadcast_to(share[None], (parts, rows, width))
    arrived = lax.all_to_all(copies, "tensor", 0, 0, tiled=True)
    return jnp.transpose(arrived, (1, 0, 2)).reshape(rows, parts * width)


def shift_pairs(shape, axis, step):
    pairs = []
    for index in range(shape[0] * shape[1] * shape[2]):
        place = [index // (shape[1] * shape[2]), (index // shape[2]) % shape[1], index % shape[2]]
        place[axis] = (place[axis] + step) % shape[axis]
        pairs.append((index, (place[0] * shape[1] + place[1]) * shape[2] + place[2]))
    return pairs


def ring_along(block, shape, axis):
    size = shape[axis]
    up = shift_pairs(shape, axis, 1)
    down = shift_pairs(shape, axis, -1)
    pieces = [block]
    from_below = block
    from_above = block
    for _ in range((size - 1) // 2):
        from_below = lax.ppermute(from_below, "seq", up)
        from_above = lax.ppermute(from_above, "seq", down)
        pieces += [from_below, from_above]
    if size % 2 == 0:
        half = block.shape[2] // 2
        first = lax.ppermute(from_below[:, :, :half], "seq", up)
        second = lax.ppermute(from_above[:, :, half:], "seq", down)
        pieces += [first, second]
    return jnp.concatenate(pieces, axis=2)


def ring_gather_seq(block, seq_size, companion, between):
    cores = 2
    lanes = 4
    shape = (seq_size // (lanes * cores), lanes, cores)
    gathered = ring_along(block, shape, 0)
    gathered, companion = lax.optimization_barrier((gathered, companion))
    companion = between(companion)
    gathered = ring_along(gathered, shape, 1)
    gathered, companion = lax.optimization_barrier((gathered, companion))
    partner = lax.ppermute(gathered, "seq", shift_pairs(shape, 2, 1))
    return jnp.concatenate([gathered, partner], axis=2), companion


def per_device(
    residual,
    query,
    new_keys,
    new_values,
    leaf_kv,
    branch_kv,
    root_kv,
    out_weight,
    norm_gain,
    norm_bias,
    up_weight,
    up_bias,
    down_weight,
    down_bias,
    segment,
    new_len,
):
    row_count = query.shape[0]
    head_count = query.shape[1] // HD
    query_heads = head_major(query, head_count)
    device = lax.axis_index("seq")
    seq_size = lax.axis_size("seq")
    parts = lax.axis_size("tensor")
    branch_count = seq_size // 4
    feature_width = branch_kv.shape[2]

    local_rows = branch_kv.shape[1] // branch_count
    branch_local = branch_kv.reshape(2, local_rows, branch_count, feature_width)
    picked = jnp.take(branch_local, segment, axis=2)
    picked = head_major(jnp.transpose(picked, (2, 0, 1, 3)), head_count)
    arrived = lax.all_to_all(picked, "seq", 0, 0, tiled=True)

    running = (
        jnp.full((head_count, row_count), NEGATIVE_FILL, jnp.float32),
        jnp.zeros((head_count, row_count), jnp.float32),
        jnp.zeros((head_count, row_count, HD), jnp.float32),
    )
    query_pos = jnp.arange(row_count, dtype=jnp.int32)
    allowed_new = (query_pos[None, :] <= query_pos[:, None]) & (
        query_pos[None, :] < new_len[device]
    )
    running = attend(
        running,
        query_heads,
        head_major(new_keys, head_count),
        head_major(new_values, head_count),
        allowed_new[None],
    )
    leaf_heads = head_major(leaf_kv, head_count)
    running = attend(running, query_heads, leaf_heads[0], leaf_heads[1], True)
    def attend_branch(companion):
        arrived, running = companion
        branch_mine = jnp.transpose(arrived, (1, 2, 0, 3, 4)).reshape(
            2, head_count, seq_size * local_rows, HD
        )
        return attend_blocks(running, query_heads, branch_mine[0], branch_mine[1])

    root_full, running = ring_gather_seq(
        head_major(root_kv, head_count), seq_size, (arrived, running), attend_branch
    )

    running = attend_blocks(running, query_heads, root_full[0], root_full[1])
    largest, totals, accumulated = running
    attention = (
        jnp.transpose(accumulated / totals[:, :, None], (1, 0, 2))
        .reshape(row_count, head_count * HD)
        .astype(jnp.bfloat16)
    )
    projected = jnp.dot(attention, out_weight, preferred_element_type=jnp.float32)
    share_width = residual.shape[1]
    column = lax.axis_index("tensor") * share_width
    mid_share = (
        tensor_sum_scatter(projected, parts) + residual.astype(jnp.float32)
    ).astype(jnp.bfloat16)
    mid_full = tensor_gather(mid_share, parts)
    wide_mid = mid_full.astype(jnp.float32)
    row_mean = jnp.mean(wide_mid, axis=1, keepdims=True)
    row_var = jnp.mean(wide_mid * wide_mid, axis=1, keepdims=True) - row_mean * row_mean
    normed = (
        (wide_mid - row_mean) * lax.rsqrt(row_var + NORM_EPSILON) * norm_gain + norm_bias
    ).astype(jnp.bfloat16)
    up_sum = jnp.dot(normed, up_weight, preferred_element_type=jnp.float32)
    hidden = lax.optimization_barrier(
        jax.nn.gelu(up_sum + up_bias, approximate=False).astype(jnp.bfloat16)
    )
    partial_value = jnp.dot(hidden, down_weight, preferred_element_type=jnp.float32)
    summed = tensor_sum_scatter(partial_value, parts)
    down_share = lax.dynamic_slice_in_dim(down_bias, column, share_width, 0)
    return (summed + down_share + mid_share.astype(jnp.float32)).astype(jnp.bfloat16)


def solution(mesh):
    return jax.shard_map(
        per_device,
        mesh=mesh,
        in_specs=(
            P("seq", "tensor"),
            P("seq", "tensor"),
            P("seq", "tensor"),
            P("seq", "tensor"),
            P(None, "seq", "tensor"),
            P(None, "seq", "tensor"),
            P(None, "seq", "tensor"),
            P("tensor", None),
            P(),
            P(),
            P(None, "tensor"),
            P("tensor"),
            P("tensor", None),
            P(),
            P(),
            P(),
        ),
        out_specs=P("seq", "tensor"),
        check_vma=False,
    )
```
